32 devices in a mesh: region: 2 (over y), mod: 4 (over z), obs: 4 (over x, core).
Axes of the slice: x: 2, y: 2, z: 4, core: 2. Of those that a mesh axis runs over, the one named last changes fastest.
Arguments:
- model_days: float32 [16384, 128], P(('region', 'mod')), parts along dimension 0, may hold values from -48 to 48
- obs_days: float32 [16384, 128], P(('region', 'obs', 'mod')), parts along dimension 0, may hold values from -48 to 48
Outputs:
- mapped: float32 [16384, 128], P(('region', 'mod', 'obs')), parts along dimension 0
- row_potential: float32 [16384], P(('region', 'mod')), parts along dimension 0
- col_potential: float32 [16384], P(('region', 'obs')), parts along dimension 0
The draws below stay inside these ranges and needn't reach their ends.
There are 2 independent parts, one for each index of `region`. The reference program is written for one: setup_inputs(seed, part) draws one part's arguments, and reference() takes and returns one part's arrays. A program takes and returns all parts, laid end to end along the dimension named above; each array names one. Nothing has to cross between parts.
All inputs are finite; a program needn't handle non-finite values.
Results may differ from the reference program's by a relative error of at most 0.0003.
Values sent between devices are 32-bit elements; how exact they have to be, the bound alone decides.
No kernel may reach another device: no remote copies, remote signals or barrier semaphores. Data moves between devices by JAX's collectives and lax.ppermute only.
A program may use at most 64 MiB of HBM per device.

```python
import math
import jax
import jax.numpy as jnp
from jax import lax

FEAT = 128
ROWS_DEV = 2048
ITERS = 2
MODEL_DAYS = 8192
OBS_DAYS = 8192
N_MOD = 4


def draw_model_days(key, part):
    base = jax.random.normal(jax.random.fold_in(key, 11), (MODEL_DAYS, FEAT), jnp.float32)
    return base


def draw_obs_days(key, part):
    base = jax.random.normal(jax.random.fold_in(key, 21), (OBS_DAYS, FEAT), jnp.float32)
    return 1.2 * base + 0.3


def setup_inputs(seed: int = 0, part: int = 0) -> dict:
    streams_of = jax.random.split(jax.random.key(seed), 3)
    own_keys = jax.random.split(jax.random.fold_in(streams_of[2], part), 3)
    model_days = draw_model_days(jax.random.fold_in(jax.random.fold_in(streams_of[2], part), 71), part)
    obs_days = draw_obs_days(jax.random.fold_in(jax.random.fold_in(streams_of[2], part), 71), part)
    return dict(model_days=model_days, obs_days=obs_days)


entropy_scale = 0.02


def pair_cost(block_rows, block_square, columns, column_square):
    cross = lax.dot_general(block_rows, columns, (((1,), (1,)), ((), ())), precision=lax.Precision.HIGHEST, preferred_element_type=jnp.float32)
    return (block_square[:, None] + column_square[None, :] - 2.0 * cross) / block_rows.shape[1]


def reference(model_days, obs_days):
    blocks = model_days.reshape(N_MOD, ROWS_DEV, FEAT)
    column_square = jnp.sum(obs_days * obs_days, axis=1)

    def scores_for(block_rows, col_potential):
        block_cost = pair_cost(block_rows, jnp.sum(block_rows * block_rows, axis=1), obs_days, column_square)
        return (col_potential[None, :] - block_cost) / entropy_scale

    def row_lse(col_potential):
        def single(block_rows):
            scores = scores_for(block_rows, col_potential)
            peaks = jnp.max(scores, axis=1)
            return peaks + jnp.log(jnp.sum(jnp.exp(scores - peaks[:, None]), axis=1))
        return lax.map(single, blocks).reshape(-1)

    def col_lse(row_potential):
        potential_blocks = row_potential.reshape(N_MOD, ROWS_DEV)

        def advance(running, inputs):
            block_rows, block_potential = inputs
            block_cost = pair_cost(block_rows, jnp.sum(block_rows * block_rows, axis=1), obs_days, column_square)
            scores = (block_potential[:, None] - block_cost) / entropy_scale
            peaks, totals = running
            new_peaks = jnp.maximum(peaks, jnp.max(scores, axis=0))
            totals = totals * jnp.exp(peaks - new_peaks) + jnp.sum(jnp.exp(scores - new_peaks[None, :]), axis=0)
            return (new_peaks, totals), None

        start = (jnp.full((OBS_DAYS,), -jnp.inf, jnp.float32), jnp.zeros((OBS_DAYS,), jnp.float32))
        (peaks, totals), _ = lax.scan(advance, start, (blocks, potential_blocks))
        return peaks + jnp.log(totals)

    col_potential = jnp.zeros((OBS_DAYS,), jnp.float32)
    for iteration in range(ITERS):
        row_potential = -entropy_scale * (row_lse(col_potential) - math.log(OBS_DAYS))
        col_potential = -entropy_scale * (col_lse(row_potential) - math.log(MODEL_DAYS))
    final_lse = row_lse(col_potential)
    row_potential = -entropy_scale * (final_lse - math.log(OBS_DAYS))

    def project(inputs):
        block_rows, block_lse = inputs
        weights = jnp.exp(scores_for(block_rows, col_potential) - block_lse[:, None])
        return jnp.dot(weights, obs_days, precision=lax.Precision.HIGHEST, preferred_element_type=jnp.float32)

    mapped = lax.map(project, (blocks, final_lse.reshape(N_MOD, ROWS_DEV))).reshape(MODEL_DAYS, FEAT)
    return (mapped, row_potential, col_potential)
```

```python
import math

import jax
import jax.numpy as jnp
from jax import lax
from jax.sharding import PartitionSpec as P

ITERS = 2


entropy_scale = 0.02


def shift_pairs(n, s):
    return [(i, (i + s) % n) for i in range(n)]


def pair_cost(block_rows, block_square, columns):
    column_square = jnp.sum(columns * columns, axis=1)
    cross = lax.dot_general(
        block_rows,
        columns,
        (((1,), (1,)), ((), ())),
        precision=lax.Precision.HIGHEST,
        preferred_element_type=jnp.float32,
    )
    return (block_square[:, None] + column_square[None, :] - 2.0 * cross) / block_rows.shape[1]


def lse_across(local_lse, axis):
    n = lax.axis_size(axis)
    vals = [local_lse] + [lax.ppermute(local_lse, axis, shift_pairs(n, s)) for s in range(1, n)]
    stacked = jnp.stack(vals)
    top = jnp.max(stacked, axis=0)
    return top + jnp.log(jnp.sum(jnp.exp(stacked - top[None]), axis=0))


def reorder(vec, order):
    n = order.shape[0]
    return jnp.take(vec.reshape(n, -1), order, axis=0).reshape(-1)


def scatter_obs(partial):
    n = lax.axis_size("obs")
    half = n // 2
    o = lax.axis_index("obs")
    x = o // 2
    c = o % 2
    share = partial.shape[0] // n
    p4 = partial.reshape(half, 2, share, partial.shape[1])
    keep = lax.dynamic_index_in_dim(p4, c, axis=1, keepdims=False)
    give = lax.dynamic_index_in_dim(p4, 1 - c, axis=1, keepdims=False)
    acc = keep + lax.ppermute(give, "obs", [(i, i ^ 1) for i in range(n)])
    total = lax.dynamic_index_in_dim(acc, x, axis=0, keepdims=False)
    for k in range(1, half):
        pairs = [(i, ((i // 2 + k) % half) * 2 + i % 2) for i in range(n)]
        piece = lax.dynamic_index_in_dim(acc, (x + k) % half, axis=0, keepdims=False)
        total = total + lax.ppermute(piece, "obs", pairs)
    return total


def on_device(model_days, obs_days):
    row_square = jnp.sum(model_days * model_days, axis=1)
    row_count = model_days.shape[0]
    n_mod = lax.axis_size("mod")
    m = lax.axis_index("mod")
    col_count = obs_days.shape[0] * n_mod
    log_obs = math.log(col_count * lax.axis_size("obs"))
    log_model = math.log(row_count * n_mod)
    blocks = [obs_days] + [
        lax.ppermute(obs_days, "mod", shift_pairs(n_mod, s)) for s in range(1, n_mod)
    ]
    order = (m - jnp.arange(n_mod)) % n_mod
    gathered = jnp.concatenate(blocks, axis=0)
    cost_tile = jnp.concatenate(
        [pair_cost(model_days, row_square, b) for b in blocks], axis=1
    )

    def row_lse(col_potential):
        scores = (col_potential[None, :] - cost_tile) / entropy_scale
        peaks = jnp.max(scores, axis=1)
        local = peaks + jnp.log(jnp.sum(jnp.exp(scores - peaks[:, None]), axis=1))
        return lse_across(local, "obs")

    col_shift = jnp.zeros((col_count,), jnp.float32)
    for iteration in range(ITERS):
        row_potential = -entropy_scale * (row_lse(col_shift) - log_obs)
        col_scores = (row_potential[:, None] - cost_tile) / entropy_scale
        col_peaks = jnp.max(col_scores, axis=0)
        local = col_peaks + jnp.log(jnp.sum(jnp.exp(col_scores - col_peaks[None, :]), axis=0))
        col_global = lse_across(reorder(local, order), "mod")
        col_potential = -entropy_scale * (col_global - log_model)
        col_shift = reorder(col_potential, order)
    final_lse = row_lse(col_shift)
    row_potential = -entropy_scale * (final_lse - log_obs)
    weights = jnp.exp((col_shift[None, :] - cost_tile) / entropy_scale - final_lse[:, None])
    partial_map = jnp.dot(
        weights, gathered, precision=lax.Precision.HIGHEST, preferred_element_type=jnp.float32
    )
    mapped = scatter_obs(partial_map)
    return (mapped, row_potential, col_potential)


def solution(mesh):
    in_specs = (P(("region", "mod"), None), P(("region", "obs", "mod"), None))
    out_specs = (P(("region", "mod", "obs"), None), P(("region", "mod")), P(("region", "obs")))
    return jax.shard_map(
        on_device, mesh=mesh, in_specs=in_specs, out_specs=out_specs, check_vma=False
    )
```

```python
import math

import jax
import jax.numpy as jnp
from jax import lax
from jax.experimental import pallas as pl
from jax.experimental.pallas import tpu as pltpu
from jax.sharding import PartitionSpec as P

ITERS = 2

INV_E = 50.0
RB = 8

def _row_kernel(h_ref, c_ref, o_ref):
    h = h_ref[...]
    tr = c_ref.shape[0]
    def body(i, carry):
        r = pl.multiple_of(i * RB, RB)
        s = (h - c_ref[pl.ds(r, RB), :]) * INV_E
        m = jnp.max(s, axis=1, keepdims=True)
        t = jnp.sum(jnp.exp(s - m), axis=1, keepdims=True)
        o_ref[pl.ds(r, RB), :] = m + jnp.log(t)
        return carry
    lax.fori_loop(0, tr // RB, body, 0)

def row_lse_local(h, cost, tr=256):
    R, C = cost.shape
    out = pl.pallas_call(
        _row_kernel,
        grid=(R // tr,),
        in_specs=[pl.BlockSpec((1, C), lambda i: (0, 0)), pl.BlockSpec((tr, C), lambda i: (i, 0))],
        out_specs=pl.BlockSpec((tr, 1), lambda i: (i, 0)),
        out_shape=jax.ShapeDtypeStruct((R, 1), jnp.float32),
    )(h.reshape(1, C), cost)
    return out.reshape(R)

CB = 32
def _col_kernel(g_ref, c_ref, o_ref):
    R, tc = c_ref.shape
    def mx(i, m):
        r = pl.multiple_of(i * CB, CB)
        s = (g_ref[pl.ds(r, CB), :] - c_ref[pl.ds(r, CB), :]) * INV_E
        return jnp.maximum(m, s)
    m8 = lax.fori_loop(0, R // CB, mx, jnp.full((CB, tc), -jnp.inf, jnp.float32))
    m = jnp.max(m8, axis=0, keepdims=True)
    def sm(i, t):
        r = pl.multiple_of(i * CB, CB)
        s = (g_ref[pl.ds(r, CB), :] - c_ref[pl.ds(r, CB), :]) * INV_E
        return t + jnp.exp(s - m)
    t8 = lax.fori_loop(0, R // CB, sm, jnp.zeros((CB, tc), jnp.float32))
    o_ref[...] = m + jnp.log(jnp.sum(t8, axis=0, keepdims=True))

def col_lse_local(g, cost, tc=256):
    R, C = cost.shape
    out = pl.pallas_call(
        _col_kernel,
        grid=(C // tc,),
        in_specs=[pl.BlockSpec((R, 1), lambda j: (0, 0)), pl.BlockSpec((R, tc), lambda j: (0, j))],
        out_specs=pl.BlockSpec((1, tc), lambda j: (0, j)),
        out_shape=jax.ShapeDtypeStruct((1, C), jnp.float32),
    )(g.reshape(R, 1), cost)
    return out.reshape(C)

FB = 8
def _final_kernel(h_ref, c_ref, y_ref, m_ref, l_ref, p_ref, w_ref):
    h = h_ref[...]
    tr = c_ref.shape[0]
    def body(i, carry):
        r = pl.multiple_of(i * FB, FB)
        s = (h - c_ref[pl.ds(r, FB), :]) * INV_E
        m = jnp.max(s, axis=1, keepdims=True)
        w = jnp.exp(s - m)
        t = jnp.sum(w, axis=1, keepdims=True)
        m_ref[pl.ds(r, FB), :] = m
        l_ref[pl.ds(r, FB), :] = m + jnp.log(t)
        w_ref[pl.ds(r, FB), :] = w
        return carry
    lax.fori_loop(0, tr // FB, body, 0)
    w = w_ref[...]
    wh = w.astype(jnp.bfloat16)
    wl = (w - wh.astype(jnp.float32)).astype(jnp.bfloat16)
    y = y_ref[...]
    yh = y.astype(jnp.bfloat16)
    yl = (y - yh.astype(jnp.float32)).astype(jnp.bfloat16)
    acc = jnp.dot(wh, yh, preferred_element_type=jnp.float32)
    acc = acc + jnp.dot(wh, yl, preferred_element_type=jnp.float32)
    acc = acc + jnp.dot(wl, yh, preferred_element_type=jnp.float32)
    p_ref[...] = acc

def final_local(h, cost, y, tr=256):
    R, C = cost.shape
    F = y.shape[1]
    m, l, p = pl.pallas_call(
        _final_kernel,
        grid=(R // tr,),
        in_specs=[pl.BlockSpec((1, C), lambda i: (0, 0)), pl.BlockSpec((tr, C), lambda i: (i, 0)),
                  pl.BlockSpec((C, F), lambda i: (0, 0))],
        out_specs=[pl.BlockSpec((tr, 1), lambda i: (i, 0)), pl.BlockSpec((tr, 1), lambda i: (i, 0)),
                   pl.BlockSpec((tr, F), lambda i: (i, 0))],
        out_shape=[jax.ShapeDtypeStruct((R, 1), jnp.float32), jax.ShapeDtypeStruct((R, 1), jnp.float32),
                   jax.ShapeDtypeStruct((R, F), jnp.float32)],
        scratch_shapes=[pltpu.VMEM((tr, C), jnp.float32)],
    )(h.reshape(1, C), cost, y)
    return m.reshape(R), l.reshape(R), p


entropy_scale = 0.02


def shift_pairs(n, s):
    return [(i, (i + s) % n) for i in range(n)]


def pair_cost(block_rows, block_square, columns):
    column_square = jnp.sum(columns * columns, axis=1)
    cross = lax.dot_general(
        block_rows,
        columns,
        (((1,), (1,)), ((), ())),
        precision=lax.Precision.HIGHEST,
        preferred_element_type=jnp.float32,
    )
    return (block_square[:, None] + column_square[None, :] - 2.0 * cross) / block_rows.shape[1]


def lse_across(local_lse, axis):
    n = lax.axis_size(axis)
    vals = [local_lse] + [lax.ppermute(local_lse, axis, shift_pairs(n, s)) for s in range(1, n)]
    stacked = jnp.stack(vals)
    top = jnp.max(stacked, axis=0)
    return top + jnp.log(jnp.sum(jnp.exp(stacked - top[None]), axis=0))


def reorder(vec, order):
    n = order.shape[0]
    return jnp.take(vec.reshape(n, -1), order, axis=0).reshape(-1)


def scatter_obs(partial):
    n = lax.axis_size("obs")
    half = n // 2
    o = lax.axis_index("obs")
    x = o // 2
    c = o % 2
    share = partial.shape[0] // n
    p4 = partial.reshape(half, 2, share, partial.shape[1])
    keep = lax.dynamic_index_in_dim(p4, c, axis=1, keepdims=False)
    give = lax.dynamic_index_in_dim(p4, 1 - c, axis=1, keepdims=False)
    acc = keep + lax.ppermute(give, "obs", [(i, i ^ 1) for i in range(n)])
    total = lax.dynamic_index_in_dim(acc, x, axis=0, keepdims=False)
    for k in range(1, half):
        pairs = [(i, ((i // 2 + k) % half) * 2 + i % 2) for i in range(n)]
        piece = lax.dynamic_index_in_dim(acc, (x + k) % half, axis=0, keepdims=False)
        total = total + lax.ppermute(piece, "obs", pairs)
    return total


def on_device(model_days, obs_days):
    row_square = jnp.sum(model_days * model_days, axis=1)
    row_count = model_days.shape[0]
    n_mod = lax.axis_size("mod")
    m = lax.axis_index("mod")
    col_count = obs_days.shape[0] * n_mod
    log_obs = math.log(col_count * lax.axis_size("obs"))
    log_model = math.log(row_count * n_mod)
    blocks = [obs_days] + [
        lax.ppermute(obs_days, "mod", shift_pairs(n_mod, s)) for s in range(1, n_mod)
    ]
    order = (m - jnp.arange(n_mod)) % n_mod
    gathered = jnp.concatenate(blocks, axis=0)
    cost_tile = jnp.concatenate(
        [pair_cost(model_days, row_square, b) for b in blocks], axis=1
    )

    col_shift = jnp.zeros((col_count,), jnp.float32)
    for iteration in range(ITERS):
        row_lse = lse_across(row_lse_local(col_shift, cost_tile), "obs")
        row_potential = -entropy_scale * (row_lse - log_obs)
        local = col_lse_local(row_potential, cost_tile)
        col_global = lse_across(reorder(local, order), "mod")
        col_potential = -entropy_scale * (col_global - log_model)
        col_shift = reorder(col_potential, order)
    peaks, local, partial_map = final_local(col_shift, cost_tile, gathered)
    final_lse = lse_across(local, "obs")
    row_potential = -entropy_scale * (final_lse - log_obs)
    mapped = scatter_obs(partial_map * jnp.exp(peaks - final_lse)[:, None])
    return (mapped, row_potential, col_potential)


def solution(mesh):
    in_specs = (P(("region", "mod"), None), P(("region", "obs", "mod"), None))
    out_specs = (P(("region", "mod", "obs"), None), P(("region", "mod")), P(("region", "obs")))
    return jax.shard_map(
        on_device, mesh=mesh, in_specs=in_specs, out_specs=out_specs, check_vma=False
    )
```

```python
import math

import jax
import jax.numpy as jnp
from jax import lax
from jax.experimental import pallas as pl
from jax.experimental.pallas import tpu as pltpu
from jax.sharding import PartitionSpec as P

ITERS = 2

INV_E = 50.0
RB = 8


def _lane_tiles(s):
    return [s[:, j * 128:(j + 1) * 128] for j in range(s.shape[1] // 128)]

def _row_pass_max(h, c_ref, m_scr, tr):
    def p1(i, carry):
        r = pl.multiple_of(i * RB, RB)
        tiles = _lane_tiles((h - c_ref[pl.ds(r, RB), :]) * INV_E)
        m = tiles[0]
        for t in tiles[1:]:
            m = jnp.maximum(m, t)
        m_scr[pl.ds(r, RB), :] = m
        return carry
    lax.fori_loop(0, tr // RB, p1, 0, unroll=4)
    return jnp.max(m_scr[...], axis=1, keepdims=True)

FB = 8
def _final_kernel(h_ref, c_ref, y_ref, m_ref, l_ref, p_ref, w_ref, m_scr, t_scr):
    h = h_ref[...]
    tr = c_ref.shape[0]
    m_ref[...] = _row_pass_max(h, c_ref, m_scr, tr)
    def p2(i, carry):
        r = pl.multiple_of(i * RB, RB)
        mr = m_ref[pl.ds(r, RB), :]
        w = jnp.exp((h - c_ref[pl.ds(r, RB), :]) * INV_E - mr)
        w_ref[pl.ds(r, RB), :] = w
        tiles = _lane_tiles(w)
        t = tiles[0]
        for u in tiles[1:]:
            t = t + u
        t_scr[pl.ds(r, RB), :] = t
        return carry
    lax.fori_loop(0, tr // RB, p2, 0, unroll=4)
    l_ref[...] = m_ref[...] + jnp.log(jnp.sum(t_scr[...], axis=1, keepdims=True))
    w = w_ref[...]
    wh = w.astype(jnp.bfloat16)
    wl = (w - wh.astype(jnp.float32)).astype(jnp.bfloat16)
    y = y_ref[...]
    yh = y.astype(jnp.bfloat16)
    yl = (y - yh.astype(jnp.float32)).astype(jnp.bfloat16)
    acc = jnp.dot(wh, yh, preferred_element_type=jnp.float32)
    acc = acc + jnp.dot(wh, yl, preferred_element_type=jnp.float32)
    acc = acc + jnp.dot(wl, yh, preferred_element_type=jnp.float32)
    p_ref[...] = acc

def final_local(h, cost, y, tr=256):
    R, C = cost.shape
    F = y.shape[1]
    m, l, p = pl.pallas_call(
        _final_kernel,
        grid=(R // tr,),
        in_specs=[pl.BlockSpec((1, C), lambda i: (0, 0)), pl.BlockSpec((tr, C), lambda i: (i, 0)),
                  pl.BlockSpec((C, F), lambda i: (0, 0))],
        out_specs=[pl.BlockSpec((tr, 1), lambda i: (i, 0)), pl.BlockSpec((tr, 1), lambda i: (i, 0)),
                   pl.BlockSpec((tr, F), lambda i: (i, 0))],
        out_shape=[jax.ShapeDtypeStruct((R, 1), jnp.float32), jax.ShapeDtypeStruct((R, 1), jnp.float32),
                   jax.ShapeDtypeStruct((R, F), jnp.float32)],
        scratch_shapes=[pltpu.VMEM((tr, C), jnp.float32), pltpu.VMEM((tr, 128), jnp.float32), pltpu.VMEM((tr, 128), jnp.float32)],
    )(h.reshape(1, C), cost, y)
    return m.reshape(R), l.reshape(R), p


entropy_scale = 0.02


def shift_pairs(n, s):
    return [(i, (i + s) % n) for i in range(n)]


def pair_cost(block_rows, block_square, columns):
    column_square = jnp.sum(columns * columns, axis=1)
    cross = lax.dot_general(
        block_rows,
        columns,
        (((1,), (1,)), ((), ())),
        precision=lax.Precision.HIGHEST,
        preferred_element_type=jnp.float32,
    )
    return (block_square[:, None] + column_square[None, :] - 2.0 * cross) / block_rows.shape[1]


def lse_across(local_lse, axis):
    n = lax.axis_size(axis)
    vals = [local_lse] + [lax.ppermute(local_lse, axis, shift_pairs(n, s)) for s in range(1, n)]
    stacked = jnp.stack(vals)
    top = jnp.max(stacked, axis=0)
    return top + jnp.log(jnp.sum(jnp.exp(stacked - top[None]), axis=0))


def reorder(vec, order):
    n = order.shape[0]
    return jnp.take(vec.reshape(n, -1), order, axis=0).reshape(-1)


def scatter_obs(partial):
    n = lax.axis_size("obs")
    half = n // 2
    o = lax.axis_index("obs")
    x = o // 2
    c = o % 2
    share = partial.shape[0] // n
    p4 = partial.reshape(half, 2, share, partial.shape[1])
    keep = lax.dynamic_index_in_dim(p4, c, axis=1, keepdims=False)
    give = lax.dynamic_index_in_dim(p4, 1 - c, axis=1, keepdims=False)
    acc = keep + lax.ppermute(give, "obs", [(i, i ^ 1) for i in range(n)])
    total = lax.dynamic_index_in_dim(acc, x, axis=0, keepdims=False)
    for k in range(1, half):
        pairs = [(i, ((i // 2 + k) % half) * 2 + i % 2) for i in range(n)]
        piece = lax.dynamic_index_in_dim(acc, (x + k) % half, axis=0, keepdims=False)
        total = total + lax.ppermute(piece, "obs", pairs)
    return total


def on_device(model_days, obs_days):
    row_square = jnp.sum(model_days * model_days, axis=1)
    row_count = model_days.shape[0]
    n_mod = lax.axis_size("mod")
    m = lax.axis_index("mod")
    col_count = obs_days.shape[0] * n_mod
    log_obs = math.log(col_count * lax.axis_size("obs"))
    log_model = math.log(row_count * n_mod)
    blocks = [obs_days] + [
        lax.ppermute(obs_days, "mod", shift_pairs(n_mod, s)) for s in range(1, n_mod)
    ]
    order = (m - jnp.arange(n_mod)) % n_mod
    gathered = jnp.concatenate(blocks, axis=0)
    cost_tile = jnp.concatenate(
        [pair_cost(model_days, row_square, b) for b in blocks], axis=1
    )

    def row_lse(col_potential):
        scores = (col_potential[None, :] - cost_tile) / entropy_scale
        peaks = jnp.max(scores, axis=1)
        local = peaks + jnp.log(jnp.sum(jnp.exp(scores - peaks[:, None]), axis=1))
        return lse_across(local, "obs")

    col_shift = jnp.zeros((col_count,), jnp.float32)
    for iteration in range(ITERS):
        row_potential = -entropy_scale * (row_lse(col_shift) - log_obs)
        col_scores = (row_potential[:, None] - cost_tile) / entropy_scale
        col_peaks = jnp.max(col_scores, axis=0)
        local = col_peaks + jnp.log(jnp.sum(jnp.exp(col_scores - col_peaks[None, :]), axis=0))
        col_global = lse_across(reorder(local, order), "mod")
        col_potential = -entropy_scale * (col_global - log_model)
        col_shift = reorder(col_potential, order)
    peaks, local, partial_map = final_local(col_shift, cost_tile, gathered)
    final_lse = lse_across(local, "obs")
    row_potential = -entropy_scale * (final_lse - log_obs)
    mapped = scatter_obs(partial_map * jnp.exp(peaks - final_lse)[:, None])
    return (mapped, row_potential, col_potential)


def solution(mesh):
    in_specs = (P(("region", "mod"), None), P(("region", "obs", "mod"), None))
    out_specs = (P(("region", "mod", "obs"), None), P(("region", "mod")), P(("region", "obs")))
    return jax.shard_map(
        on_device, mesh=mesh, in_specs=in_specs, out_specs=out_specs, check_vma=False
    )
```

```python
import math

import jax
import jax.numpy as jnp
from jax import lax
from jax.experimental import pallas as pl
from jax.experimental.pallas import tpu as pltpu
from jax.sharding import PartitionSpec as P

ITERS = 2

RB = 8


def _lane_tiles(s):
    return [s[:, j * 128:(j + 1) * 128] for j in range(s.shape[1] // 128)]

def _row_pass_max(h, c_ref, m_scr, tr):
    def p1(i, carry):
        r = pl.multiple_of(i * RB, RB)
        tiles = _lane_tiles(h + c_ref[pl.ds(r, RB), :])
        m = tiles[0]
        for t in tiles[1:]:
            m = jnp.maximum(m, t)
        m_scr[pl.ds(r, RB), :] = m
        return carry
    lax.fori_loop(0, tr // RB, p1, 0, unroll=4)
    return jnp.max(m_scr[...], axis=1, keepdims=True)

FB = 8
def _final_kernel(h_ref, c_ref, y_ref, m_ref, l_ref, p_ref, w_ref, m_scr, t_scr):
    h = h_ref[...]
    tr = c_ref.shape[0]
    m_ref[...] = _row_pass_max(h, c_ref, m_scr, tr)
    def p2(i, carry):
        r = pl.multiple_of(i * RB, RB)
        mr = m_ref[pl.ds(r, RB), :]
        w = jnp.exp((h + c_ref[pl.ds(r, RB), :]) - mr)
        w_ref[pl.ds(r, RB), :] = w
        tiles = _lane_tiles(w)
        t = tiles[0]
        for u in tiles[1:]:
            t = t + u
        t_scr[pl.ds(r, RB), :] = t
        return carry
    lax.fori_loop(0, tr // RB, p2, 0, unroll=4)
    l_ref[...] = m_ref[...] + jnp.log(jnp.sum(t_scr[...], axis=1, keepdims=True))
    w = w_ref[...]
    wh = w.astype(jnp.bfloat16)
    wl = (w - wh.astype(jnp.float32)).astype(jnp.bfloat16)
    y = y_ref[...]
    yh = y.astype(jnp.bfloat16)
    yl = (y - yh.astype(jnp.float32)).astype(jnp.bfloat16)
    acc = jnp.dot(wh, yh, preferred_element_type=jnp.float32)
    acc = acc + jnp.dot(wh, yl, preferred_element_type=jnp.float32)
    acc = acc + jnp.dot(wl, yh, preferred_element_type=jnp.float32)
    p_ref[...] = acc

def final_local(h, cost, y, tr=256):
    R, C = cost.shape
    F = y.shape[1]
    m, l, p = pl.pallas_call(
        _final_kernel,
        grid=(R // tr,),
        in_specs=[pl.BlockSpec((1, C), lambda i: (0, 0)), pl.BlockSpec((tr, C), lambda i: (i, 0)),
                  pl.BlockSpec((C, F), lambda i: (0, 0))],
        out_specs=[pl.BlockSpec((tr, 1), lambda i: (i, 0)), pl.BlockSpec((tr, 1), lambda i: (i, 0)),
                   pl.BlockSpec((tr, F), lambda i: (i, 0))],
        out_shape=[jax.ShapeDtypeStruct((R, 1), jnp.float32), jax.ShapeDtypeStruct((R, 1), jnp.float32),
                   jax.ShapeDtypeStruct((R, F), jnp.float32)],
        scratch_shapes=[pltpu.VMEM((tr, C), jnp.float32), pltpu.VMEM((tr, 128), jnp.float32), pltpu.VMEM((tr, 128), jnp.float32)],
    )(h.reshape(1, C), cost, y)
    return m.reshape(R), l.reshape(R), p


entropy_scale = 0.02


def shift_pairs(n, s):
    return [(i, (i + s) % n) for i in range(n)]


def pair_scores(block_rows, block_square, columns):
    column_square = jnp.sum(columns * columns, axis=1)
    cross = lax.dot_general(
        block_rows,
        columns,
        (((1,), (1,)), ((), ())),
        precision=lax.Precision.HIGHEST,
        preferred_element_type=jnp.float32,
    )
    cost = (block_square[:, None] + column_square[None, :] - 2.0 * cross) / block_rows.shape[1]
    return -cost / entropy_scale


def lse_across(local_lse, axis):
    n = lax.axis_size(axis)
    vals = [local_lse] + [lax.ppermute(local_lse, axis, shift_pairs(n, s)) for s in range(1, n)]
    stacked = jnp.stack(vals)
    top = jnp.max(stacked, axis=0)
    return top + jnp.log(jnp.sum(jnp.exp(stacked - top[None]), axis=0))


def reorder(vec, order):
    n = order.shape[0]
    return jnp.take(vec.reshape(n, -1), order, axis=0).reshape(-1)


def scatter_obs(partial):
    n = lax.axis_size("obs")
    half = n // 2
    o = lax.axis_index("obs")
    x = o // 2
    c = o % 2
    share = partial.shape[0] // n
    p4 = partial.reshape(half, 2, share, partial.shape[1])
    keep = lax.dynamic_index_in_dim(p4, c, axis=1, keepdims=False)
    give = lax.dynamic_index_in_dim(p4, 1 - c, axis=1, keepdims=False)
    acc = keep + lax.ppermute(give, "obs", [(i, i ^ 1) for i in range(n)])
    total = lax.dynamic_index_in_dim(acc, x, axis=0, keepdims=False)
    for k in range(1, half):
        pairs = [(i, ((i // 2 + k) % half) * 2 + i % 2) for i in range(n)]
        piece = lax.dynamic_index_in_dim(acc, (x + k) % half, axis=0, keepdims=False)
        total = total + lax.ppermute(piece, "obs", pairs)
    return total


def on_device(model_days, obs_days):
    row_square = jnp.sum(model_days * model_days, axis=1)
    row_count = model_days.shape[0]
    n_mod = lax.axis_size("mod")
    m = lax.axis_index("mod")
    col_count = obs_days.shape[0] * n_mod
    log_obs = math.log(col_count * lax.axis_size("obs"))
    log_model = math.log(row_count * n_mod)
    blocks = [obs_days] + [
        lax.ppermute(obs_days, "mod", shift_pairs(n_mod, s)) for s in range(1, n_mod)
    ]
    order = (m - jnp.arange(n_mod)) % n_mod
    gathered = jnp.concatenate(blocks, axis=0)
    base_tile = jnp.concatenate(
        [pair_scores(model_days, row_square, b) for b in blocks], axis=1
    )

    def row_lse(col_potential):
        scores = (col_potential / entropy_scale)[None, :] + base_tile
        peaks = jnp.max(scores, axis=1)
        local = peaks + jnp.log(jnp.sum(jnp.exp(scores - peaks[:, None]), axis=1))
        return lse_across(local, "obs")

    col_shift = jnp.zeros((col_count,), jnp.float32)
    for iteration in range(ITERS):
        row_potential = -entropy_scale * (row_lse(col_shift) - log_obs)
        col_scores = (row_potential / entropy_scale)[:, None] + base_tile
        col_peaks = jnp.max(col_scores, axis=0)
        local = col_peaks + jnp.log(jnp.sum(jnp.exp(col_scores - col_peaks[None, :]), axis=0))
        col_global = lse_across(reorder(local, order), "mod")
        col_potential = -entropy_scale * (col_global - log_model)
        col_shift = reorder(col_potential, order)
    peaks, local, partial_map = final_local(col_shift / entropy_scale, base_tile, gathered)
    final_lse = lse_across(local, "obs")
    row_potential = -entropy_scale * (final_lse - log_obs)
    mapped = scatter_obs(partial_map * jnp.exp(peaks - final_lse)[:, None])
    return (mapped, row_potential, col_potential)


def solution(mesh):
    in_specs = (P(("region", "mod"), None), P(("region", "obs", "mod"), None))
    out_specs = (P(("region", "mod", "obs"), None), P(("region", "mod")), P(("region", "obs")))
    return jax.shard_map(
        on_device, mesh=mesh, in_specs=in_specs, out_specs=out_specs, check_vma=False
    )
```

```python
import math

import jax
import jax.numpy as jnp
from jax import lax
from jax.experimental import pallas as pl
from jax.experimental.pallas import tpu as pltpu
from jax.sharding import PartitionSpec as P

ITERS = 2

RB = 8


def _lane_tiles(s):
    return [s[:, j * 128:(j + 1) * 128] for j in range(s.shape[1] // 128)]

def _row_pass_max(h, c_ref, m_scr, tr):
    def p1(i, carry):
        r = pl.multiple_of(i * RB, RB)
        tiles = _lane_tiles(h + c_ref[pl.ds(r, RB), :])
        m = tiles[0]
        for t in tiles[1:]:
            m = jnp.maximum(m, t)
        m_scr[pl.ds(r, RB), :] = m
        return carry
    lax.fori_loop(0, tr // RB, p1, 0, unroll=4)
    return jnp.max(m_scr[...], axis=1, keepdims=True)

FB = 8
def _final_kernel(h_ref, c_ref, y_ref, m_ref, l_ref, p_ref, w_ref, m_scr, t_scr):
    h = h_ref[...]
    tr = c_ref.shape[0]
    m_ref[...] = _row_pass_max(h, c_ref, m_scr, tr)
    def p2(i, carry):
        r = pl.multiple_of(i * RB, RB)
        mr = m_ref[pl.ds(r, RB), :]
        w = jnp.exp((h + c_ref[pl.ds(r, RB), :]) - mr)
        w_ref[pl.ds(r, RB), :] = w
        tiles = _lane_tiles(w)
        t = tiles[0]
        for u in tiles[1:]:
            t = t + u
        t_scr[pl.ds(r, RB), :] = t
        return carry
    lax.fori_loop(0, tr // RB, p2, 0, unroll=4)
    l_ref[...] = m_ref[...] + jnp.log(jnp.sum(t_scr[...], axis=1, keepdims=True))
    w = w_ref[...]
    wh = w.astype(jnp.bfloat16)
    wl = (w - wh.astype(jnp.float32)).astype(jnp.bfloat16)
    y = y_ref[...]
    yh = y.astype(jnp.bfloat16)
    yl = (y - yh.astype(jnp.float32)).astype(jnp.bfloat16)
    acc = jnp.dot(wh, yh, preferred_element_type=jnp.float32)
    acc = acc + jnp.dot(wh, yl, preferred_element_type=jnp.float32)
    acc = acc + jnp.dot(wl, yh, preferred_element_type=jnp.float32)
    p_ref[...] = acc

def final_local(h, cost, y, tr=256):
    R, C = cost.shape
    F = y.shape[1]
    m, l, p = pl.pallas_call(
        _final_kernel,
        grid=(R // tr,),
        in_specs=[pl.BlockSpec((1, C), lambda i: (0, 0)), pl.BlockSpec((tr, C), lambda i: (i, 0)),
                  pl.BlockSpec((C, F), lambda i: (0, 0))],
        out_specs=[pl.BlockSpec((tr, 1), lambda i: (i, 0)), pl.BlockSpec((tr, 1), lambda i: (i, 0)),
                   pl.BlockSpec((tr, F), lambda i: (i, 0))],
        out_shape=[jax.ShapeDtypeStruct((R, 1), jnp.float32), jax.ShapeDtypeStruct((R, 1), jnp.float32),
                   jax.ShapeDtypeStruct((R, F), jnp.float32)],
        scratch_shapes=[pltpu.VMEM((tr, C), jnp.float32), pltpu.VMEM((tr, 128), jnp.float32), pltpu.VMEM((tr, 128), jnp.float32)],
    )(h.reshape(1, C), cost, y)
    return m.reshape(R), l.reshape(R), p


entropy_scale = 0.02


def shift_pairs(n, s):
    return [(i, (i + s) % n) for i in range(n)]


def pair_scores(block_rows, block_square, columns):
    column_square = jnp.sum(columns * columns, axis=1)
    cross = lax.dot_general(
        block_rows,
        columns,
        (((1,), (1,)), ((), ())),
        precision=lax.Precision.HIGHEST,
        preferred_element_type=jnp.float32,
    )
    cost = (block_square[:, None] + column_square[None, :] - 2.0 * cross) / block_rows.shape[1]
    return -cost / entropy_scale


def lse_across(local_lse, axis):
    n = lax.axis_size(axis)
    vals = [local_lse] + [lax.ppermute(local_lse, axis, shift_pairs(n, s)) for s in range(1, n)]
    stacked = jnp.stack(vals)
    top = jnp.max(stacked, axis=0)
    return top + jnp.log(jnp.sum(jnp.exp(stacked - top[None]), axis=0))


def reorder(vec, order):
    n = order.shape[0]
    return jnp.take(vec.reshape(n, -1), order, axis=0).reshape(-1)


def scatter_obs(partial, peaks, final_lse):
    n = lax.axis_size("obs")
    half = n // 2
    o = lax.axis_index("obs")
    x = o // 2
    c = o % 2
    share = partial.shape[0] // n
    p4 = partial.reshape(half, 2, share, partial.shape[1])
    m4 = peaks.reshape(half, 2, share)
    keep = lax.dynamic_index_in_dim(p4, c, axis=1, keepdims=False)
    give = lax.dynamic_index_in_dim(p4, 1 - c, axis=1, keepdims=False)
    m_keep = lax.dynamic_index_in_dim(m4, c, axis=1, keepdims=False)
    m_give = lax.dynamic_index_in_dim(m4, 1 - c, axis=1, keepdims=False)
    partner = [(i, i ^ 1) for i in range(n)]
    got = lax.ppermute(give, "obs", partner)
    m_got = lax.ppermute(m_give, "obs", partner)
    top = jnp.maximum(m_keep, m_got)
    acc = keep * jnp.exp(m_keep - top)[..., None] + got * jnp.exp(m_got - top)[..., None]
    pieces = [(lax.dynamic_index_in_dim(acc, x, axis=0, keepdims=False),
               lax.dynamic_index_in_dim(top, x, axis=0, keepdims=False))]
    for k in range(1, half):
        pairs = [(i, ((i // 2 + k) % half) * 2 + i % 2) for i in range(n)]
        j = (x + k) % half
        pieces.append((
            lax.ppermute(lax.dynamic_index_in_dim(acc, j, axis=0, keepdims=False), "obs", pairs),
            lax.ppermute(lax.dynamic_index_in_dim(top, j, axis=0, keepdims=False), "obs", pairs),
        ))
    own_lse = lax.dynamic_slice_in_dim(final_lse, o * share, share)
    total = pieces[0][0] * jnp.exp(pieces[0][1] - own_lse)[:, None]
    for piece, piece_top in pieces[1:]:
        total = total + piece * jnp.exp(piece_top - own_lse)[:, None]
    return total


def on_device(model_days, obs_days):
    row_square = jnp.sum(model_days * model_days, axis=1)
    row_count = model_days.shape[0]
    n_mod = lax.axis_size("mod")
    m = lax.axis_index("mod")
    col_count = obs_days.shape[0] * n_mod
    log_obs = math.log(col_count * lax.axis_size("obs"))
    log_model = math.log(row_count * n_mod)
    blocks = [obs_days] + [
        lax.ppermute(obs_days, "mod", shift_pairs(n_mod, s)) for s in range(1, n_mod)
    ]
    order = (m - jnp.arange(n_mod)) % n_mod
    gathered = jnp.concatenate(blocks, axis=0)
    base_tile = jnp.concatenate(
        [pair_scores(model_days, row_square, b) for b in blocks], axis=1
    )

    def row_lse(col_potential):
        scores = (col_potential / entropy_scale)[None, :] + base_tile
        peaks = jnp.max(scores, axis=1)
        local = peaks + jnp.log(jnp.sum(jnp.exp(scores - peaks[:, None]), axis=1))
        return lse_across(local, "obs")

    col_shift = jnp.zeros((col_count,), jnp.float32)
    for iteration in range(ITERS):
        row_potential = -entropy_scale * (row_lse(col_shift) - log_obs)
        col_scores = (row_potential / entropy_scale)[:, None] + base_tile
        col_peaks = jnp.max(col_scores, axis=0)
        local = col_peaks + jnp.log(jnp.sum(jnp.exp(col_scores - col_peaks[None, :]), axis=0))
        col_global = lse_across(reorder(local, order), "mod")
        col_potential = -entropy_scale * (col_global - log_model)
        col_shift = reorder(col_potential, order)
    peaks, local, partial_map = final_local(col_shift / entropy_scale, base_tile, gathered)
    final_lse = lse_across(local, "obs")
    row_potential = -entropy_scale * (final_lse - log_obs)
    mapped = scatter_obs(partial_map, peaks, final_lse)
    return (mapped, row_potential, col_potential)


def solution(mesh):
    in_specs = (P(("region", "mod"), None), P(("region", "obs", "mod"), None))
    out_specs = (P(("region", "mod", "obs"), None), P(("region", "mod")), P(("region", "obs")))
    return jax.shard_map(
        on_device, mesh=mesh, in_specs=in_specs, out_specs=out_specs, check_vma=False
    )
```

```python
import math

import jax
import jax.numpy as jnp
from jax import lax
from jax.experimental import pallas as pl
from jax.experimental.pallas import tpu as pltpu
from jax.sharding import PartitionSpec as P

ITERS = 2

RB = 8


def _lane_tiles(s):
    return [s[:, j * 128:(j + 1) * 128] for j in range(s.shape[1] // 128)]


def _final_kernel(*refs):
    h_ref = refs[0]
    nb = len(refs) - 8
    c_refs = refs[1:1 + nb]
    y_ref, m_ref, l_ref, p_ref, w_ref, m_scr, t_scr = refs[1 + nb:]
    tr = c_refs[0].shape[0]
    width = c_refs[0].shape[1]

    def scores(r):
        return [h_ref[:, k * width:(k + 1) * width] + c[pl.ds(r, RB), :] for k, c in enumerate(c_refs)]

    def p1(i, carry):
        r = pl.multiple_of(i * RB, RB)
        tiles = [t for sc in scores(r) for t in _lane_tiles(sc)]
        m = tiles[0]
        for t in tiles[1:]:
            m = jnp.maximum(m, t)
        m_scr[pl.ds(r, RB), :] = m
        return carry
    lax.fori_loop(0, tr // RB, p1, 0, unroll=4)
    m_ref[...] = jnp.max(m_scr[...], axis=1, keepdims=True)

    def p2(i, carry):
        r = pl.multiple_of(i * RB, RB)
        mr = m_ref[pl.ds(r, RB), :]
        t = None
        for k, sc in enumerate(scores(r)):
            w = jnp.exp(sc - mr)
            w_ref[pl.ds(r, RB), k * width:(k + 1) * width] = w
            for u in _lane_tiles(w):
                t = u if t is None else t + u
        t_scr[pl.ds(r, RB), :] = t
        return carry
    lax.fori_loop(0, tr // RB, p2, 0, unroll=4)
    l_ref[...] = m_ref[...] + jnp.log(jnp.sum(t_scr[...], axis=1, keepdims=True))
    w = w_ref[...]
    wh = w.astype(jnp.bfloat16)
    wl = (w - wh.astype(jnp.float32)).astype(jnp.bfloat16)
    y = y_ref[...]
    yh = y.astype(jnp.bfloat16)
    yl = (y - yh.astype(jnp.float32)).astype(jnp.bfloat16)
    acc = jnp.dot(wh, yh, preferred_element_type=jnp.float32)
    acc = acc + jnp.dot(wh, yl, preferred_element_type=jnp.float32)
    acc = acc + jnp.dot(wl, yh, preferred_element_type=jnp.float32)
    p_ref[...] = acc


def final_local(h, blocks, y, tr=256):
    R, width = blocks[0].shape
    C = width * len(blocks)
    F = y.shape[1]
    m, l, p = pl.pallas_call(
        _final_kernel,
        grid=(R // tr,),
        in_specs=[pl.BlockSpec((1, C), lambda i: (0, 0))]
        + [pl.BlockSpec((tr, width), lambda i: (i, 0)) for _ in blocks]
        + [pl.BlockSpec((C, F), lambda i: (0, 0))],
        out_specs=[pl.BlockSpec((tr, 1), lambda i: (i, 0)), pl.BlockSpec((tr, 1), lambda i: (i, 0)),
                   pl.BlockSpec((tr, F), lambda i: (i, 0))],
        out_shape=[jax.ShapeDtypeStruct((R, 1), jnp.float32), jax.ShapeDtypeStruct((R, 1), jnp.float32),
                   jax.ShapeDtypeStruct((R, F), jnp.float32)],
        scratch_shapes=[pltpu.VMEM((tr, C), jnp.float32), pltpu.VMEM((tr, 128), jnp.float32),
                        pltpu.VMEM((tr, 128), jnp.float32)],
    )(h.reshape(1, C), *blocks, y)
    return m.reshape(R), l.reshape(R), p


entropy_scale = 0.02


def shift_pairs(n, s):
    return [(i, (i + s) % n) for i in range(n)]


def pair_scores(block_rows, block_square, columns):
    column_square = jnp.sum(columns * columns, axis=1)
    cross = lax.dot_general(
        block_rows,
        columns,
        (((1,), (1,)), ((), ())),
        precision=lax.Precision.HIGHEST,
        preferred_element_type=jnp.float32,
    )
    cost = (block_square[:, None] + column_square[None, :] - 2.0 * cross) / block_rows.shape[1]
    return -cost / entropy_scale


def lse_across(local_lse, axis):
    n = lax.axis_size(axis)
    vals = [local_lse] + [lax.ppermute(local_lse, axis, shift_pairs(n, s)) for s in range(1, n)]
    stacked = jnp.stack(vals)
    top = jnp.max(stacked, axis=0)
    return top + jnp.log(jnp.sum(jnp.exp(stacked - top[None]), axis=0))


def reorder(vec, order):
    n = order.shape[0]
    return jnp.take(vec.reshape(n, -1), order, axis=0).reshape(-1)


def scatter_obs(partial, peaks, final_lse):
    n = lax.axis_size("obs")
    half = n // 2
    o = lax.axis_index("obs")
    x = o // 2
    c = o % 2
    share = partial.shape[0] // n
    p4 = partial.reshape(half, 2, share, partial.shape[1])
    m4 = peaks.reshape(half, 2, share)
    keep = lax.dynamic_index_in_dim(p4, c, axis=1, keepdims=False)
    give = lax.dynamic_index_in_dim(p4, 1 - c, axis=1, keepdims=False)
    m_keep = lax.dynamic_index_in_dim(m4, c, axis=1, keepdims=False)
    m_give = lax.dynamic_index_in_dim(m4, 1 - c, axis=1, keepdims=False)
    partner = [(i, i ^ 1) for i in range(n)]
    got = lax.ppermute(give, "obs", partner)
    m_got = lax.ppermute(m_give, "obs", partner)
    top = jnp.maximum(m_keep, m_got)
    acc = keep * jnp.exp(m_keep - top)[..., None] + got * jnp.exp(m_got - top)[..., None]
    pieces = [(lax.dynamic_index_in_dim(acc, x, axis=0, keepdims=False),
               lax.dynamic_index_in_dim(top, x, axis=0, keepdims=False))]
    for k in range(1, half):
        pairs = [(i, ((i // 2 + k) % half) * 2 + i % 2) for i in range(n)]
        j = (x + k) % half
        pieces.append((
            lax.ppermute(lax.dynamic_index_in_dim(acc, j, axis=0, keepdims=False), "obs", pairs),
            lax.ppermute(lax.dynamic_index_in_dim(top, j, axis=0, keepdims=False), "obs", pairs),
        ))
    own_lse = lax.dynamic_slice_in_dim(final_lse, o * share, share)
    total = pieces[0][0] * jnp.exp(pieces[0][1] - own_lse)[:, None]
    for piece, piece_top in pieces[1:]:
        total = total + piece * jnp.exp(piece_top - own_lse)[:, None]
    return total


def on_device(model_days, obs_days):
    row_square = jnp.sum(model_days * model_days, axis=1)
    row_count = model_days.shape[0]
    n_mod = lax.axis_size("mod")
    m = lax.axis_index("mod")
    col_count = obs_days.shape[0] * n_mod
    log_obs = math.log(col_count * lax.axis_size("obs"))
    log_model = math.log(row_count * n_mod)
    blocks = [obs_days] + [
        lax.ppermute(obs_days, "mod", shift_pairs(n_mod, s)) for s in range(1, n_mod)
    ]
    order = (m - jnp.arange(n_mod)) % n_mod
    gathered = jnp.concatenate(blocks, axis=0)
    base_blocks = [pair_scores(model_days, row_square, b) for b in blocks]

    def split(vec):
        return jnp.split(vec, n_mod)

    def row_lse(col_potential):
        parts = []
        for hb, sb in zip(split(col_potential / entropy_scale), base_blocks):
            scores = hb[None, :] + sb
            peaks = jnp.max(scores, axis=1)
            parts.append(peaks + jnp.log(jnp.sum(jnp.exp(scores - peaks[:, None]), axis=1)))
        stacked = jnp.stack(parts)
        top = jnp.max(stacked, axis=0)
        local = top + jnp.log(jnp.sum(jnp.exp(stacked - top[None]), axis=0))
        return lse_across(local, "obs")

    def col_lse(row_potential):
        g = (row_potential / entropy_scale)[:, None]
        parts = []
        for sb in base_blocks:
            col_scores = g + sb
            col_peaks = jnp.max(col_scores, axis=0)
            parts.append(col_peaks + jnp.log(jnp.sum(jnp.exp(col_scores - col_peaks[None, :]), axis=0)))
        return jnp.concatenate(parts)

    col_shift = jnp.zeros((col_count,), jnp.float32)
    for iteration in range(ITERS):
        row_potential = -entropy_scale * (row_lse(col_shift) - log_obs)
        local = col_lse(row_potential)
        col_global = lse_across(reorder(local, order), "mod")
        col_potential = -entropy_scale * (col_global - log_model)
        col_shift = reorder(col_potential, order)
    peaks, local, partial_map = final_local(col_shift / entropy_scale, base_blocks, gathered)
    final_lse = lse_across(local, "obs")
    row_potential = -entropy_scale * (final_lse - log_obs)
    mapped = scatter_obs(partial_map, peaks, final_lse)
    return (mapped, row_potential, col_potential)


def solution(mesh):
    in_specs = (P(("region", "mod"), None), P(("region", "obs", "mod"), None))
    out_specs = (P(("region", "mod", "obs"), None), P(("region", "mod")), P(("region", "obs")))
    return jax.shard_map(
        on_device, mesh=mesh, in_specs=in_specs, out_specs=out_specs, check_vma=False
    )
```

```python
import math

import jax
import jax.numpy as jnp
from jax import lax
from jax.experimental import pallas as pl
from jax.experimental.pallas import tpu as pltpu
from jax.sharding import PartitionSpec as P

ITERS = 2

RB = 8


def _lane_tiles(s):
    return [s[:, j * 128:(j + 1) * 128] for j in range(s.shape[1] // 128)]


def _final_kernel(*refs):
    h_ref = refs[0]
    nb = len(refs) - 8
    c_refs = refs[1:1 + nb]
    y_ref, m_ref, l_ref, p_ref, w_ref, m_scr, t_scr = refs[1 + nb:]
    tr = c_refs[0].shape[0]
    width = c_refs[0].shape[1]

    def scores(r):
        return [h_ref[:, k * width:(k + 1) * width] + c[pl.ds(r, RB), :] for k, c in enumerate(c_refs)]

    def p1(i, carry):
        r = pl.multiple_of(i * RB, RB)
        tiles = [t for sc in scores(r) for t in _lane_tiles(sc)]
        m = tiles[0]
        for t in tiles[1:]:
            m = jnp.maximum(m, t)
        m_scr[pl.ds(r, RB), :] = m
        return carry
    lax.fori_loop(0, tr // RB, p1, 0, unroll=4)
    m_ref[...] = jnp.max(m_scr[...], axis=1, keepdims=True)

    def p2(i, carry):
        r = pl.multiple_of(i * RB, RB)
        mr = m_ref[pl.ds(r, RB), :]
        t = None
        for k, sc in enumerate(scores(r)):
            w = jnp.exp(sc - mr)
            w_ref[pl.ds(r, RB), k * width:(k + 1) * width] = w
            for u in _lane_tiles(w):
                t = u if t is None else t + u
        t_scr[pl.ds(r, RB), :] = t
        return carry
    lax.fori_loop(0, tr // RB, p2, 0, unroll=4)
    l_ref[...] = m_ref[...] + jnp.log(jnp.sum(t_scr[...], axis=1, keepdims=True))
    w = w_ref[...]
    wh = w.astype(jnp.bfloat16)
    wl = (w - wh.astype(jnp.float32)).astype(jnp.bfloat16)
    y = y_ref[...]
    yh = y.astype(jnp.bfloat16)
    yl = (y - yh.astype(jnp.float32)).astype(jnp.bfloat16)
    acc = jnp.dot(wh, yh, preferred_element_type=jnp.float32)
    acc = acc + jnp.dot(wh, yl, preferred_element_type=jnp.float32)
    acc = acc + jnp.dot(wl, yh, preferred_element_type=jnp.float32)
    p_ref[...] = acc


def final_local(h, blocks, y, tr=256):
    R, width = blocks[0].shape
    C = width * len(blocks)
    F = y.shape[1]
    m, l, p = pl.pallas_call(
        _final_kernel,
        grid=(R // tr,),
        in_specs=[pl.BlockSpec((1, C), lambda i: (0, 0))]
        + [pl.BlockSpec((tr, width), lambda i: (i, 0)) for _ in blocks]
        + [pl.BlockSpec((C, F), lambda i: (0, 0))],
        out_specs=[pl.BlockSpec((tr, 1), lambda i: (i, 0)), pl.BlockSpec((tr, 1), lambda i: (i, 0)),
                   pl.BlockSpec((tr, F), lambda i: (i, 0))],
        out_shape=[jax.ShapeDtypeStruct((R, 1), jnp.float32), jax.ShapeDtypeStruct((R, 1), jnp.float32),
                   jax.ShapeDtypeStruct((R, F), jnp.float32)],
        scratch_shapes=[pltpu.VMEM((tr, C), jnp.float32), pltpu.VMEM((tr, 128), jnp.float32),
                        pltpu.VMEM((tr, 128), jnp.float32)],
    )(h.reshape(1, C), *blocks, y)
    return m.reshape(R), l.reshape(R), p


entropy_scale = 0.02


def shift_pairs(n, s):
    return [(i, (i + s) % n) for i in range(n)]


def pair_scores(block_rows, block_square, columns):
    column_square = jnp.sum(columns * columns, axis=1)
    cross = lax.dot_general(
        block_rows,
        columns,
        (((1,), (1,)), ((), ())),
        precision=lax.Precision.HIGHEST,
        preferred_element_type=jnp.float32,
    )
    cost = (block_square[:, None] + column_square[None, :] - 2.0 * cross) / block_rows.shape[1]
    return -cost / entropy_scale


def lse_across(local_lse, axis):
    n = lax.axis_size(axis)
    vals = [local_lse] + [lax.ppermute(local_lse, axis, shift_pairs(n, s)) for s in range(1, n)]
    stacked = jnp.stack(vals)
    top = jnp.max(stacked, axis=0)
    return top + jnp.log(jnp.sum(jnp.exp(stacked - top[None]), axis=0))


def reorder(vec, order):
    n = order.shape[0]
    return jnp.take(vec.reshape(n, -1), order, axis=0).reshape(-1)


def scatter_obs(partial, peaks, final_lse):
    n = lax.axis_size("obs")
    half = n // 2
    o = lax.axis_index("obs")
    x = o // 2
    c = o % 2
    share = partial.shape[0] // n
    p4 = partial.reshape(half, 2, share, partial.shape[1])
    m4 = peaks.reshape(half, 2, share)
    keep = lax.dynamic_index_in_dim(p4, c, axis=1, keepdims=False)
    give = lax.dynamic_index_in_dim(p4, 1 - c, axis=1, keepdims=False)
    m_keep = lax.dynamic_index_in_dim(m4, c, axis=1, keepdims=False)
    m_give = lax.dynamic_index_in_dim(m4, 1 - c, axis=1, keepdims=False)
    partner = [(i, i ^ 1) for i in range(n)]
    got = lax.ppermute(give, "obs", partner)
    m_got = lax.ppermute(m_give, "obs", partner)
    top = jnp.maximum(m_keep, m_got)
    acc = keep * jnp.exp(m_keep - top)[..., None] + got * jnp.exp(m_got - top)[..., None]
    pieces = [(lax.dynamic_index_in_dim(acc, x, axis=0, keepdims=False),
               lax.dynamic_index_in_dim(top, x, axis=0, keepdims=False))]
    for k in range(1, half):
        pairs = [(i, ((i // 2 + k) % half) * 2 + i % 2) for i in range(n)]
        j = (x + k) % half
        pieces.append((
            lax.ppermute(lax.dynamic_index_in_dim(acc, j, axis=0, keepdims=False), "obs", pairs),
            lax.ppermute(lax.dynamic_index_in_dim(top, j, axis=0, keepdims=False), "obs", pairs),
        ))
    own_lse = lax.dynamic_slice_in_dim(final_lse, o * share, share)
    total = pieces[0][0] * jnp.exp(pieces[0][1] - own_lse)[:, None]
    for piece, piece_top in pieces[1:]:
        total = total + piece * jnp.exp(piece_top - own_lse)[:, None]
    return total


def on_device(model_days, obs_days):
    row_square = jnp.sum(model_days * model_days, axis=1)
    row_count = model_days.shape[0]
    n_mod = lax.axis_size("mod")
    m = lax.axis_index("mod")
    col_count = obs_days.shape[0] * n_mod
    log_obs = math.log(col_count * lax.axis_size("obs"))
    log_model = math.log(row_count * n_mod)
    blocks = [obs_days] + [
        lax.ppermute(obs_days, "mod", shift_pairs(n_mod, s)) for s in range(1, n_mod)
    ]
    order = (m - jnp.arange(n_mod)) % n_mod
    gathered = jnp.concatenate(blocks, axis=0)
    base_blocks = [pair_scores(model_days, row_square, b) for b in blocks]

    def split(vec):
        return jnp.split(vec, n_mod)

    def row_lse(col_potential):
        parts = []
        for hb, sb in zip(split(col_potential / entropy_scale), base_blocks):
            scores = hb[None, :] + sb
            peaks = jnp.max(scores, axis=1)
            parts.append(peaks + jnp.log(jnp.sum(jnp.exp(scores - peaks[:, None]), axis=1)))
        stacked = jnp.stack(parts)
        top = jnp.max(stacked, axis=0)
        local = top + jnp.log(jnp.sum(jnp.exp(stacked - top[None]), axis=0))
        return lse_across(local, "obs")

    def col_lse(row_potential):
        g = (row_potential / entropy_scale)[:, None]
        parts = []
        for sb in base_blocks:
            col_scores = g + sb
            col_peaks = jnp.max(col_scores, axis=0)
            parts.append(col_peaks + jnp.log(jnp.sum(jnp.exp(col_scores - col_peaks[None, :]), axis=0)))
        return jnp.concatenate(parts)

    def iterate(iteration, carry):
        col_shift, _ = carry
        row_potential = -entropy_scale * (row_lse(col_shift) - log_obs)
        local = col_lse(row_potential)
        col_global = lse_across(reorder(local, order), "mod")
        col_potential = -entropy_scale * (col_global - log_model)
        return reorder(col_potential, order), col_potential

    zeros = jnp.zeros((col_count,), jnp.float32)
    col_shift, col_potential = lax.fori_loop(0, ITERS, iterate, (zeros, zeros))
    peaks, local, partial_map = final_local(col_shift / entropy_scale, base_blocks, gathered)
    final_lse = lse_across(local, "obs")
    row_potential = -entropy_scale * (final_lse - log_obs)
    mapped = scatter_obs(partial_map, peaks, final_lse)
    return (mapped, row_potential, col_potential)


def solution(mesh):
    in_specs = (P(("region", "mod"), None), P(("region", "obs", "mod"), None))
    out_specs = (P(("region", "mod", "obs"), None), P(("region", "mod")), P(("region", "obs")))
    return jax.shard_map(
        on_device, mesh=mesh, in_specs=in_specs, out_specs=out_specs, check_vma=False
    )
```

```python
import math

import jax
import jax.numpy as jnp
from jax import lax
from jax.experimental import pallas as pl
from jax.experimental.pallas import tpu as pltpu
from jax.sharding import PartitionSpec as P

ITERS = 2

RB = 8


def _lane_tiles(s):
    return [s[:, j * 128:(j + 1) * 128] for j in range(s.shape[1] // 128)]


def _final_kernel(*refs):
    h_ref = refs[0]
    nb = len(refs) - 8
    c_refs = refs[1:1 + nb]
    y_ref, m_ref, l_ref, p_ref, w_ref, m_scr, t_scr = refs[1 + nb:]
    tr = c_refs[0].shape[0]
    width = c_refs[0].shape[1]

    def scores(r):
        return [h_ref[:, k * width:(k + 1) * width] + c[pl.ds(r, RB), :] for k, c in enumerate(c_refs)]

    def p1(i, carry):
        r = pl.multiple_of(i * RB, RB)
        tiles = [t for sc in scores(r) for t in _lane_tiles(sc)]
        m = tiles[0]
        for t in tiles[1:]:
            m = jnp.maximum(m, t)
        m_scr[pl.ds(r, RB), :] = m
        return carry
    lax.fori_loop(0, tr // RB, p1, 0, unroll=4)
    m_ref[...] = jnp.max(m_scr[...], axis=1, keepdims=True)

    def p2(i, carry):
        r = pl.multiple_of(i * RB, RB)
        mr = m_ref[pl.ds(r, RB), :]
        t = None
        for k, sc in enumerate(scores(r)):
            w = jnp.exp(sc - mr)
            w_ref[pl.ds(r, RB), k * width:(k + 1) * width] = w
            for u in _lane_tiles(w):
                t = u if t is None else t + u
        t_scr[pl.ds(r, RB), :] = t
        return carry
    lax.fori_loop(0, tr // RB, p2, 0, unroll=4)
    l_ref[...] = m_ref[...] + jnp.log(jnp.sum(t_scr[...], axis=1, keepdims=True))
    w = w_ref[...]
    wh = w.astype(jnp.bfloat16)
    wl = (w - wh.astype(jnp.float32)).astype(jnp.bfloat16)
    y = y_ref[...]
    yh = y.astype(jnp.bfloat16)
    yl = (y - yh.astype(jnp.float32)).astype(jnp.bfloat16)
    acc = jnp.dot(wh, yh, preferred_element_type=jnp.float32)
    acc = acc + jnp.dot(wh, yl, preferred_element_type=jnp.float32)
    acc = acc + jnp.dot(wl, yh, preferred_element_type=jnp.float32)
    p_ref[...] = acc


def final_local(h, blocks, y, tr=256):
    R, width = blocks[0].shape
    C = width * len(blocks)
    F = y.shape[1]
    m, l, p = pl.pallas_call(
        _final_kernel,
        grid=(R // tr,),
        in_specs=[pl.BlockSpec((1, C), lambda i: (0, 0))]
        + [pl.BlockSpec((tr, width), lambda i: (i, 0)) for _ in blocks]
        + [pl.BlockSpec((C, F), lambda i: (0, 0))],
        out_specs=[pl.BlockSpec((tr, 1), lambda i: (i, 0)), pl.BlockSpec((tr, 1), lambda i: (i, 0)),
                   pl.BlockSpec((tr, F), lambda i: (i, 0))],
        out_shape=[jax.ShapeDtypeStruct((R, 1), jnp.float32), jax.ShapeDtypeStruct((R, 1), jnp.float32),
                   jax.ShapeDtypeStruct((R, F), jnp.float32)],
        scratch_shapes=[pltpu.VMEM((tr, C), jnp.float32), pltpu.VMEM((tr, 128), jnp.float32),
                        pltpu.VMEM((tr, 128), jnp.float32)],
    )(h.reshape(1, C), *blocks, y)
    return m.reshape(R), l.reshape(R), p


entropy_scale = 0.02


def shift_pairs(n, s):
    return [(i, (i + s) % n) for i in range(n)]


def pair_scores(block_rows, block_square, columns):
    column_square = jnp.sum(columns * columns, axis=1)
    cross = lax.dot_general(
        block_rows,
        columns,
        (((1,), (1,)), ((), ())),
        precision=lax.Precision.HIGHEST,
        preferred_element_type=jnp.float32,
    )
    cost = (block_square[:, None] + column_square[None, :] - 2.0 * cross) / block_rows.shape[1]
    return -cost / entropy_scale


def lse_across(local_lse, axis):
    n = lax.axis_size(axis)
    vals = [local_lse] + [lax.ppermute(local_lse, axis, shift_pairs(n, s)) for s in range(1, n)]
    stacked = jnp.stack(vals)
    top = jnp.max(stacked, axis=0)
    return top + jnp.log(jnp.sum(jnp.exp(stacked - top[None]), axis=0))


def reorder(vec, order):
    n = order.shape[0]
    return jnp.take(vec.reshape(n, -1), order, axis=0).reshape(-1)


def scatter_obs(partial, peaks, final_lse):
    n = lax.axis_size("obs")
    half = n // 2
    o = lax.axis_index("obs")
    x = o // 2
    c = o % 2
    share = partial.shape[0] // n
    p4 = partial.reshape(half, 2, share, partial.shape[1])
    m4 = peaks.reshape(half, 2, share)
    keep = lax.dynamic_index_in_dim(p4, c, axis=1, keepdims=False)
    give = lax.dynamic_index_in_dim(p4, 1 - c, axis=1, keepdims=False)
    m_keep = lax.dynamic_index_in_dim(m4, c, axis=1, keepdims=False)
    m_give = lax.dynamic_index_in_dim(m4, 1 - c, axis=1, keepdims=False)
    partner = [(i, i ^ 1) for i in range(n)]
    got = lax.ppermute(give, "obs", partner)
    m_got = lax.ppermute(m_give, "obs", partner)
    top = jnp.maximum(m_keep, m_got)
    acc = keep * jnp.exp(m_keep - top)[..., None] + got * jnp.exp(m_got - top)[..., None]
    pieces = [(lax.dynamic_index_in_dim(acc, x, axis=0, keepdims=False),
               lax.dynamic_index_in_dim(top, x, axis=0, keepdims=False))]
    for k in range(1, half):
        pairs = [(i, ((i // 2 + k) % half) * 2 + i % 2) for i in range(n)]
        j = (x + k) % half
        pieces.append((
            lax.ppermute(lax.dynamic_index_in_dim(acc, j, axis=0, keepdims=False), "obs", pairs),
            lax.ppermute(lax.dynamic_index_in_dim(top, j, axis=0, keepdims=False), "obs", pairs),
        ))
    own_lse = lax.dynamic_slice_in_dim(final_lse, o * share, share)
    total = pieces[0][0] * jnp.exp(pieces[0][1] - own_lse)[:, None]
    for piece, piece_top in pieces[1:]:
        total = total + piece * jnp.exp(piece_top - own_lse)[:, None]
    return total


def on_device(model_days, obs_days):
    row_square = jnp.sum(model_days * model_days, axis=1)
    row_count = model_days.shape[0]
    n_mod = lax.axis_size("mod")
    m = lax.axis_index("mod")
    col_count = obs_days.shape[0] * n_mod
    log_obs = math.log(col_count * lax.axis_size("obs"))
    log_model = math.log(row_count * n_mod)
    blocks = [obs_days] + [
        lax.ppermute(obs_days, "mod", shift_pairs(n_mod, s)) for s in range(1, n_mod)
    ]
    order = (m - jnp.arange(n_mod)) % n_mod
    gathered = jnp.concatenate(blocks, axis=0)
    groups = [jnp.concatenate(blocks[:n_mod // 2], axis=0), jnp.concatenate(blocks[n_mod // 2:], axis=0)]
    base_blocks = [pair_scores(model_days, row_square, b) for b in groups]

    def split(vec):
        return jnp.split(vec, len(base_blocks))

    def row_lse(col_potential):
        parts = []
        for hb, sb in zip(split(col_potential / entropy_scale), base_blocks):
            scores = hb[None, :] + sb
            peaks = jnp.max(scores, axis=1)
            parts.append(peaks + jnp.log(jnp.sum(jnp.exp(scores - peaks[:, None]), axis=1)))
        stacked = jnp.stack(parts)
        top = jnp.max(stacked, axis=0)
        local = top + jnp.log(jnp.sum(jnp.exp(stacked - top[None]), axis=0))
        return lse_across(local, "obs")

    def col_lse(row_potential):
        g = (row_potential / entropy_scale)[:, None]
        parts = []
        for sb in base_blocks:
            col_scores = g + sb
            col_peaks = jnp.max(col_scores, axis=0)
            parts.append(col_peaks + jnp.log(jnp.sum(jnp.exp(col_scores - col_peaks[None, :]), axis=0)))
        return jnp.concatenate(parts)

    col_shift = jnp.zeros((col_count,), jnp.float32)
    for iteration in range(ITERS):
        row_potential = -entropy_scale * (row_lse(col_shift) - log_obs)
        local = col_lse(row_potential)
        col_global = lse_across(reorder(local, order), "mod")
        col_potential = -entropy_scale * (col_global - log_model)
        col_shift = reorder(col_potential, order)
    peaks, local, partial_map = final_local(col_shift / entropy_scale, base_blocks, gathered)
    final_lse = lse_across(local, "obs")
    row_potential = -entropy_scale * (final_lse - log_obs)
    mapped = scatter_obs(partial_map, peaks, final_lse)
    return (mapped, row_potential, col_potential)


def solution(mesh):
    in_specs = (P(("region", "mod"), None), P(("region", "obs", "mod"), None))
    out_specs = (P(("region", "mod", "obs"), None), P(("region", "mod")), P(("region", "obs")))
    return jax.shard_map(
        on_device, mesh=mesh, in_specs=in_specs, out_specs=out_specs, check_vma=False
    )
```

```python
import math

import jax
import jax.numpy as jnp
from jax import lax
from jax.experimental import pallas as pl
from jax.experimental.pallas import tpu as pltpu
from jax.sharding import PartitionSpec as P

ITERS = 2

RB = 8


def _lane_tiles(s):
    return [s[:, j * 128:(j + 1) * 128] for j in range(s.shape[1] // 128)]


def _final_kernel(*refs):
    h_ref = refs[1]
    nb = len(refs) - 9
    c_refs = refs[2:2 + nb]
    y_ref, m_ref, l_ref, p_ref, w_ref, m_scr, t_scr = refs[2 + nb:]
    tr = c_refs[0].shape[0]
    width = c_refs[0].shape[1]

    def scores(r):
        return [h_ref[:, k * width:(k + 1) * width] + c[pl.ds(r, RB), :] for k, c in enumerate(c_refs)]

    def p1(i, carry):
        r = pl.multiple_of(i * RB, RB)
        tiles = [t for sc in scores(r) for t in _lane_tiles(sc)]
        m = tiles[0]
        for t in tiles[1:]:
            m = jnp.maximum(m, t)
        m_scr[pl.ds(r, RB), :] = m
        return carry
    lax.fori_loop(0, tr // RB, p1, 0, unroll=4)
    m_ref[...] = jnp.max(m_scr[...], axis=1, keepdims=True)

    def p2(i, carry):
        r = pl.multiple_of(i * RB, RB)
        mr = m_ref[pl.ds(r, RB), :]
        t = None
        for k, sc in enumerate(scores(r)):
            w = jnp.exp(sc - mr)
            w_ref[pl.ds(r, RB), k * width:(k + 1) * width] = w
            for u in _lane_tiles(w):
                t = u if t is None else t + u
        t_scr[pl.ds(r, RB), :] = t
        return carry
    lax.fori_loop(0, tr // RB, p2, 0, unroll=4)
    l_ref[...] = m_ref[...] + jnp.log(jnp.sum(t_scr[...], axis=1, keepdims=True))
    w = w_ref[...]
    wh = w.astype(jnp.bfloat16)
    wl = (w - wh.astype(jnp.float32)).astype(jnp.bfloat16)
    y = y_ref[...]
    yh = y.astype(jnp.bfloat16)
    yl = (y - yh.astype(jnp.float32)).astype(jnp.bfloat16)
    acc = jnp.dot(wh, yh, preferred_element_type=jnp.float32)
    acc = acc + jnp.dot(wh, yl, preferred_element_type=jnp.float32)
    acc = acc + jnp.dot(wl, yh, preferred_element_type=jnp.float32)
    p_ref[...] = acc


def final_rows(h, blocks, y, table, tr):
    R, width = blocks[0].shape
    C = width * len(blocks)
    F = y.shape[1]
    rows = table.shape[0] * tr
    grid_spec = pltpu.PrefetchScalarGridSpec(
        num_scalar_prefetch=1,
        grid=(table.shape[0],),
        in_specs=[pl.BlockSpec((1, C), lambda i, t: (0, 0))]
        + [pl.BlockSpec((tr, width), lambda i, t: (t[i], 0)) for _ in blocks]
        + [pl.BlockSpec((C, F), lambda i, t: (0, 0))],
        out_specs=[pl.BlockSpec((tr, 1), lambda i, t: (i, 0)), pl.BlockSpec((tr, 1), lambda i, t: (i, 0)),
                   pl.BlockSpec((tr, F), lambda i, t: (i, 0))],
        scratch_shapes=[pltpu.VMEM((tr, C), jnp.float32), pltpu.VMEM((tr, 128), jnp.float32),
                        pltpu.VMEM((tr, 128), jnp.float32)],
    )
    m, l, p = pl.pallas_call(
        _final_kernel,
        grid_spec=grid_spec,
        out_shape=[jax.ShapeDtypeStruct((rows, 1), jnp.float32), jax.ShapeDtypeStruct((rows, 1), jnp.float32),
                   jax.ShapeDtypeStruct((rows, F), jnp.float32)],
    )(table, h.reshape(1, C), *blocks, y)
    return m.reshape(rows), l.reshape(rows), p


entropy_scale = 0.02


def shift_pairs(n, s):
    return [(i, (i + s) % n) for i in range(n)]


def pair_scores(block_rows, block_square, columns):
    column_square = jnp.sum(columns * columns, axis=1)
    cross = lax.dot_general(
        block_rows,
        columns,
        (((1,), (1,)), ((), ())),
        precision=lax.Precision.HIGHEST,
        preferred_element_type=jnp.float32,
    )
    cost = (block_square[:, None] + column_square[None, :] - 2.0 * cross) / block_rows.shape[1]
    return -cost / entropy_scale


def lse_across(local_lse, axis):
    n = lax.axis_size(axis)
    vals = [local_lse] + [lax.ppermute(local_lse, axis, shift_pairs(n, s)) for s in range(1, n)]
    stacked = jnp.stack(vals)
    top = jnp.max(stacked, axis=0)
    return top + jnp.log(jnp.sum(jnp.exp(stacked - top[None]), axis=0))


def reorder(vec, order):
    n = order.shape[0]
    return jnp.take(vec.reshape(n, -1), order, axis=0).reshape(-1)


def final_and_scatter(h, blocks, y, log_obs, tr=256):
    n = lax.axis_size("obs")
    half = n // 2
    o = lax.axis_index("obs")
    x = o // 2
    c = o % 2
    R = blocks[0].shape[0]
    rows_chip = R // half
    share = R // n
    per_chip = rows_chip // tr
    steps = jnp.arange(per_chip, dtype=jnp.int32)
    chips = [(x + k) % half for k in range(half)]
    partner = [(i, i ^ 1) for i in range(n)]

    def pair_sum(p_chip, m_chip):
        p2 = p_chip.reshape(2, share, p_chip.shape[1])
        m2 = m_chip.reshape(2, share)
        keep = lax.dynamic_index_in_dim(p2, c, axis=0, keepdims=False)
        give = lax.dynamic_index_in_dim(p2, 1 - c, axis=0, keepdims=False)
        m_keep = lax.dynamic_index_in_dim(m2, c, axis=0, keepdims=False)
        m_give = lax.dynamic_index_in_dim(m2, 1 - c, axis=0, keepdims=False)
        got = lax.ppermute(give, "obs", partner)
        m_got = lax.ppermute(m_give, "obs", partner)
        top = jnp.maximum(m_keep, m_got)
        return keep * jnp.exp(m_keep - top)[:, None] + got * jnp.exp(m_got - top)[:, None], top

    table = jnp.concatenate([chips[k] * per_chip + steps for k in range(1, half)]).astype(jnp.int32)
    m_far, l_far, p_far = final_rows(h, blocks, y, table, tr)
    far = [pair_sum(p_far[(k - 1) * rows_chip:k * rows_chip], m_far[(k - 1) * rows_chip:k * rows_chip])
           for k in range(1, half)]
    far, blocks, h = lax.optimization_barrier((far, blocks, h))
    pieces = []
    for k in range(1, half):
        acc, top = far[k - 1]
        pairs = [(i, ((i // 2 + k) % half) * 2 + i % 2) for i in range(n)]
        pieces.append((lax.ppermute(acc, "obs", pairs), lax.ppermute(top, "obs", pairs)))
    own_rows = final_rows(h, blocks, y, (chips[0] * per_chip + steps).astype(jnp.int32), tr)
    pieces, own_rows = lax.optimization_barrier((pieces, own_rows))
    m_own, l_own, p_own = own_rows
    l_parts = [l_own] + [l_far[(k - 1) * rows_chip:k * rows_chip] for k in range(1, half)]
    back = (jnp.arange(half) - x) % half
    local = jnp.take(jnp.stack(l_parts), back, axis=0).reshape(-1)
    final_lse = lse_across(local, "obs")
    own, own_top = pair_sum(p_own, m_own)
    own_lse = lax.dynamic_slice_in_dim(final_lse, o * share, share)
    total = own * jnp.exp(own_top - own_lse)[:, None]
    for piece, piece_top in pieces:
        total = total + piece * jnp.exp(piece_top - own_lse)[:, None]
    row_potential = -entropy_scale * (final_lse - log_obs)
    return total, row_potential


def on_device(model_days, obs_days):
    row_square = jnp.sum(model_days * model_days, axis=1)
    row_count = model_days.shape[0]
    n_mod = lax.axis_size("mod")
    m = lax.axis_index("mod")
    col_count = obs_days.shape[0] * n_mod
    log_obs = math.log(col_count * lax.axis_size("obs"))
    log_model = math.log(row_count * n_mod)
    blocks = [obs_days] + [
        lax.ppermute(obs_days, "mod", shift_pairs(n_mod, s)) for s in range(1, n_mod)
    ]
    order = (m - jnp.arange(n_mod)) % n_mod
    gathered = jnp.concatenate(blocks, axis=0)
    base_blocks = [pair_scores(model_days, row_square, b) for b in blocks]

    def split(vec):
        return jnp.split(vec, n_mod)

    def row_lse(col_potential):
        parts = []
        for hb, sb in zip(split(col_potential / entropy_scale), base_blocks):
            scores = hb[None, :] + sb
            peaks = jnp.max(scores, axis=1)
            parts.append(peaks + jnp.log(jnp.sum(jnp.exp(scores - peaks[:, None]), axis=1)))
        stacked = jnp.stack(parts)
        top = jnp.max(stacked, axis=0)
        local = top + jnp.log(jnp.sum(jnp.exp(stacked - top[None]), axis=0))
        return lse_across(local, "obs")

    def col_lse(row_potential):
        g = (row_potential / entropy_scale)[:, None]
        parts = []
        for sb in base_blocks:
            col_scores = g + sb
            col_peaks = jnp.max(col_scores, axis=0)
            parts.append(col_peaks + jnp.log(jnp.sum(jnp.exp(col_scores - col_peaks[None, :]), axis=0)))
        return jnp.concatenate(parts)

    col_shift = jnp.zeros((col_count,), jnp.float32)
    for iteration in range(ITERS):
        row_potential = -entropy_scale * (row_lse(col_shift) - log_obs)
        local = col_lse(row_potential)
        col_global = lse_across(reorder(local, order), "mod")
        col_potential = -entropy_scale * (col_global - log_model)
        col_shift = reorder(col_potential, order)
    mapped, row_potential = final_and_scatter(col_shift / entropy_scale, base_blocks, gathered, log_obs)
    return (mapped, row_potential, col_potential)


def solution(mesh):
    in_specs = (P(("region", "mod"), None), P(("region", "obs", "mod"), None))
    out_specs = (P(("region", "mod", "obs"), None), P(("region", "mod")), P(("region", "obs")))
    return jax.shard_map(
        on_device, mesh=mesh, in_specs=in_specs, out_specs=out_specs, check_vma=False
    )
```

```python
import math

import jax
import jax.numpy as jnp
from jax import lax
from jax.experimental import pallas as pl
from jax.experimental.pallas import tpu as pltpu
from jax.sharding import PartitionSpec as P

ITERS = 2

RB = 8


def _lane_tiles(s):
    return [s[:, j * 128:(j + 1) * 128] for j in range(s.shape[1] // 128)]


def _map_kernel(*refs):
    h_ref, l_ref = refs[0], refs[1]
    nb = len(refs) - 5
    c_refs = refs[2:2 + nb]
    y_ref, p_ref, w_ref = refs[2 + nb:]
    tr = c_refs[0].shape[0]
    width = c_refs[0].shape[1]

    def body(i, carry):
        r = pl.multiple_of(i * RB, RB)
        lr = l_ref[pl.ds(r, RB), :]
        for k, c in enumerate(c_refs):
            w_ref[pl.ds(r, RB), k * width:(k + 1) * width] = jnp.exp(
                (h_ref[:, k * width:(k + 1) * width] + c[pl.ds(r, RB), :]) - lr)
        return carry
    lax.fori_loop(0, tr // RB, body, 0, unroll=4)
    w = w_ref[...]
    wh = w.astype(jnp.bfloat16)
    wl = (w - wh.astype(jnp.float32)).astype(jnp.bfloat16)
    y = y_ref[...]
    yh = y.astype(jnp.bfloat16)
    yl = (y - yh.astype(jnp.float32)).astype(jnp.bfloat16)
    acc = jnp.dot(wh, yh, preferred_element_type=jnp.float32)
    acc = acc + jnp.dot(wh, yl, preferred_element_type=jnp.float32)
    acc = acc + jnp.dot(wl, yh, preferred_element_type=jnp.float32)
    p_ref[...] = acc


def map_local(h, lse, blocks, y, tr=256):
    R, width = blocks[0].shape
    C = width * len(blocks)
    F = y.shape[1]
    return pl.pallas_call(
        _map_kernel,
        grid=(R // tr,),
        in_specs=[pl.BlockSpec((1, C), lambda i: (0, 0)), pl.BlockSpec((tr, 1), lambda i: (i, 0))]
        + [pl.BlockSpec((tr, width), lambda i: (i, 0)) for _ in blocks]
        + [pl.BlockSpec((C, F), lambda i: (0, 0))],
        out_specs=pl.BlockSpec((tr, F), lambda i: (i, 0)),
        out_shape=jax.ShapeDtypeStruct((R, F), jnp.float32),
        scratch_shapes=[pltpu.VMEM((tr, C), jnp.float32)],
    )(h.reshape(1, C), lse.reshape(R, 1), *blocks, y)


entropy_scale = 0.02


def shift_pairs(n, s):
    return [(i, (i + s) % n) for i in range(n)]


def pair_scores(block_rows, block_square, columns):
    column_square = jnp.sum(columns * columns, axis=1)
    cross = lax.dot_general(
        block_rows,
        columns,
        (((1,), (1,)), ((), ())),
        precision=lax.Precision.HIGHEST,
        preferred_element_type=jnp.float32,
    )
    cost = (block_square[:, None] + column_square[None, :] - 2.0 * cross) / block_rows.shape[1]
    return -cost / entropy_scale


def lse_across(local_lse, axis):
    n = lax.axis_size(axis)
    vals = [local_lse] + [lax.ppermute(local_lse, axis, shift_pairs(n, s)) for s in range(1, n)]
    stacked = jnp.stack(vals)
    top = jnp.max(stacked, axis=0)
    return top + jnp.log(jnp.sum(jnp.exp(stacked - top[None]), axis=0))


def reorder(vec, order):
    n = order.shape[0]
    return jnp.take(vec.reshape(n, -1), order, axis=0).reshape(-1)


def scatter_obs(partial):
    n = lax.axis_size("obs")
    half = n // 2
    o = lax.axis_index("obs")
    x = o // 2
    c = o % 2
    share = partial.shape[0] // n
    p4 = partial.reshape(half, 2, share, partial.shape[1])
    keep = lax.dynamic_index_in_dim(p4, c, axis=1, keepdims=False)
    give = lax.dynamic_index_in_dim(p4, 1 - c, axis=1, keepdims=False)
    acc = keep + lax.ppermute(give, "obs", [(i, i ^ 1) for i in range(n)])
    total = lax.dynamic_index_in_dim(acc, x, axis=0, keepdims=False)
    for k in range(1, half):
        pairs = [(i, ((i // 2 + k) % half) * 2 + i % 2) for i in range(n)]
        piece = lax.dynamic_index_in_dim(acc, (x + k) % half, axis=0, keepdims=False)
        total = total + lax.ppermute(piece, "obs", pairs)
    return total


def on_device(model_days, obs_days):
    row_square = jnp.sum(model_days * model_days, axis=1)
    row_count = model_days.shape[0]
    n_mod = lax.axis_size("mod")
    m = lax.axis_index("mod")
    col_count = obs_days.shape[0] * n_mod
    log_obs = math.log(col_count * lax.axis_size("obs"))
    log_model = math.log(row_count * n_mod)
    blocks = [obs_days] + [
        lax.ppermute(obs_days, "mod", shift_pairs(n_mod, s)) for s in range(1, n_mod)
    ]
    order = (m - jnp.arange(n_mod)) % n_mod
    gathered = jnp.concatenate(blocks, axis=0)
    base_blocks = [pair_scores(model_days, row_square, b) for b in blocks]

    def split(vec):
        return jnp.split(vec, n_mod)

    def row_lse(col_potential):
        parts = []
        for hb, sb in zip(split(col_potential / entropy_scale), base_blocks):
            scores = hb[None, :] + sb
            peaks = jnp.max(scores, axis=1)
            parts.append(peaks + jnp.log(jnp.sum(jnp.exp(scores - peaks[:, None]), axis=1)))
        stacked = jnp.stack(parts)
        top = jnp.max(stacked, axis=0)
        local = top + jnp.log(jnp.sum(jnp.exp(stacked - top[None]), axis=0))
        return lse_across(local, "obs")

    def col_lse(row_potential):
        g = (row_potential / entropy_scale)[:, None]
        parts = []
        for sb in base_blocks:
            col_scores = g + sb
            col_peaks = jnp.max(col_scores, axis=0)
            parts.append(col_peaks + jnp.log(jnp.sum(jnp.exp(col_scores - col_peaks[None, :]), axis=0)))
        return jnp.concatenate(parts)

    first_lse = row_lse(jnp.zeros((col_count,), jnp.float32))

    def iterate(iteration, carry):
        lse, _, _ = carry
        row_potential = -entropy_scale * (lse - log_obs)
        local = col_lse(row_potential)
        col_global = lse_across(reorder(local, order), "mod")
        col_potential = -entropy_scale * (col_global - log_model)
        col_shift = reorder(col_potential, order)
        return row_lse(col_shift), col_potential, col_shift

    zeros = jnp.zeros((col_count,), jnp.float32)
    final_lse, col_potential, col_shift = lax.fori_loop(0, ITERS, iterate, (first_lse, zeros, zeros))
    row_potential = -entropy_scale * (final_lse - log_obs)
    mapped = scatter_obs(map_local(col_shift / entropy_scale, final_lse, base_blocks, gathered))
    return (mapped, row_potential, col_potential)


def solution(mesh):
    in_specs = (P(("region", "mod"), None), P(("region", "obs", "mod"), None))
    out_specs = (P(("region", "mod", "obs"), None), P(("region", "mod")), P(("region", "obs")))
    return jax.shard_map(
        on_device, mesh=mesh, in_specs=in_specs, out_specs=out_specs, check_vma=False
    )
```

```python
import math

import jax
import jax.numpy as jnp
from jax import lax
from jax.experimental import pallas as pl
from jax.experimental.pallas import tpu as pltpu
from jax.sharding import PartitionSpec as P

ITERS = 2

RB = 8


def _lane_tiles(s):
    return [s[:, j * 128:(j + 1) * 128] for j in range(s.shape[1] // 128)]


def _final_kernel(*refs):
    h_ref = refs[0]
    nb = len(refs) - 8
    c_refs = refs[1:1 + nb]
    y_ref, m_ref, l_ref, p_ref, w_ref, m_scr, t_scr = refs[1 + nb:]
    tr = c_refs[0].shape[0]
    width = c_refs[0].shape[1]

    def scores(r):
        return [h_ref[:, k * width:(k + 1) * width] + c[pl.ds(r, RB), :] for k, c in enumerate(c_refs)]

    def p1(i, carry):
        r = pl.multiple_of(i * RB, RB)
        tiles = [t for sc in scores(r) for t in _lane_tiles(sc)]
        m = tiles[0]
        for t in tiles[1:]:
            m = jnp.maximum(m, t)
        m_scr[pl.ds(r, RB), :] = m
        return carry
    lax.fori_loop(0, tr // RB, p1, 0, unroll=4)
    m_ref[...] = jnp.max(m_scr[...], axis=1, keepdims=True)

    def p2(i, carry):
        r = pl.multiple_of(i * RB, RB)
        mr = m_ref[pl.ds(r, RB), :]
        t = None
        for k, sc in enumerate(scores(r)):
            w = jnp.exp(sc - mr)
            w_ref[pl.ds(r, RB), k * width:(k + 1) * width] = w
            for u in _lane_tiles(w):
                t = u if t is None else t + u
        t_scr[pl.ds(r, RB), :] = t
        return carry
    lax.fori_loop(0, tr // RB, p2, 0, unroll=4)
    l_ref[...] = m_ref[...] + jnp.log(jnp.sum(t_scr[...], axis=1, keepdims=True))
    w = w_ref[...]
    wh = w.astype(jnp.bfloat16)
    wl = (w - wh.astype(jnp.float32)).astype(jnp.bfloat16)
    y = y_ref[...]
    yh = y.astype(jnp.bfloat16)
    yl = (y - yh.astype(jnp.float32)).astype(jnp.bfloat16)
    acc = jnp.dot(wh, yh, preferred_element_type=jnp.float32)
    acc = acc + jnp.dot(wh, yl, preferred_element_type=jnp.float32)
    acc = acc + jnp.dot(wl, yh, preferred_element_type=jnp.float32)
    p_ref[...] = acc


def final_local(h, blocks, y, tr=256):
    R, width = blocks[0].shape
    C = width * len(blocks)
    F = y.shape[1]
    m, l, p = pl.pallas_call(
        _final_kernel,
        grid=(R // tr,),
        in_specs=[pl.BlockSpec((1, C), lambda i: (0, 0))]
        + [pl.BlockSpec((tr, width), lambda i: (i, 0)) for _ in blocks]
        + [pl.BlockSpec((C, F), lambda i: (0, 0))],
        out_specs=[pl.BlockSpec((tr, 1), lambda i: (i, 0)), pl.BlockSpec((tr, 1), lambda i: (i, 0)),
                   pl.BlockSpec((tr, F), lambda i: (i, 0))],
        out_shape=[jax.ShapeDtypeStruct((R, 1), jnp.float32), jax.ShapeDtypeStruct((R, 1), jnp.float32),
                   jax.ShapeDtypeStruct((R, F), jnp.float32)],
        scratch_shapes=[pltpu.VMEM((tr, C), jnp.float32), pltpu.VMEM((tr, 128), jnp.float32),
                        pltpu.VMEM((tr, 128), jnp.float32)],
    )(h.reshape(1, C), *blocks, y)
    return m.reshape(R), l.reshape(R), p


entropy_scale = 0.02


def shift_pairs(n, s):
    return [(i, (i + s) % n) for i in range(n)]


def pair_scores(block_rows, block_square, columns):
    column_square = jnp.sum(columns * columns, axis=1)
    cross = lax.dot_general(
        block_rows,
        columns,
        (((1,), (1,)), ((), ())),
        precision=lax.Precision.HIGH,
        preferred_element_type=jnp.float32,
    )
    cost = (block_square[:, None] + column_square[None, :] - 2.0 * cross) / block_rows.shape[1]
    return -cost / entropy_scale


def lse_across(local_lse, axis):
    n = lax.axis_size(axis)
    vals = [local_lse] + [lax.ppermute(local_lse, axis, shift_pairs(n, s)) for s in range(1, n)]
    stacked = jnp.stack(vals)
    top = jnp.max(stacked, axis=0)
    return top + jnp.log(jnp.sum(jnp.exp(stacked - top[None]), axis=0))


def reorder(vec, order):
    n = order.shape[0]
    return jnp.take(vec.reshape(n, -1), order, axis=0).reshape(-1)


def scatter_obs(partial, peaks, final_lse):
    n = lax.axis_size("obs")
    half = n // 2
    o = lax.axis_index("obs")
    x = o // 2
    c = o % 2
    share = partial.shape[0] // n
    p4 = partial.reshape(half, 2, share, partial.shape[1])
    m4 = peaks.reshape(half, 2, share)
    keep = lax.dynamic_index_in_dim(p4, c, axis=1, keepdims=False)
    give = lax.dynamic_index_in_dim(p4, 1 - c, axis=1, keepdims=False)
    m_keep = lax.dynamic_index_in_dim(m4, c, axis=1, keepdims=False)
    m_give = lax.dynamic_index_in_dim(m4, 1 - c, axis=1, keepdims=False)
    partner = [(i, i ^ 1) for i in range(n)]
    got = lax.ppermute(give, "obs", partner)
    m_got = lax.ppermute(m_give, "obs", partner)
    top = jnp.maximum(m_keep, m_got)
    acc = keep * jnp.exp(m_keep - top)[..., None] + got * jnp.exp(m_got - top)[..., None]
    pieces = [(lax.dynamic_index_in_dim(acc, x, axis=0, keepdims=False),
               lax.dynamic_index_in_dim(top, x, axis=0, keepdims=False))]
    for k in range(1, half):
        pairs = [(i, ((i // 2 + k) % half) * 2 + i % 2) for i in range(n)]
        j = (x + k) % half
        pieces.append((
            lax.ppermute(lax.dynamic_index_in_dim(acc, j, axis=0, keepdims=False), "obs", pairs),
            lax.ppermute(lax.dynamic_index_in_dim(top, j, axis=0, keepdims=False), "obs", pairs),
        ))
    own_lse = lax.dynamic_slice_in_dim(final_lse, o * share, share)
    total = pieces[0][0] * jnp.exp(pieces[0][1] - own_lse)[:, None]
    for piece, piece_top in pieces[1:]:
        total = total + piece * jnp.exp(piece_top - own_lse)[:, None]
    return total


def on_device(model_days, obs_days):
    row_square = jnp.sum(model_days * model_days, axis=1)
    row_count = model_days.shape[0]
    n_mod = lax.axis_size("mod")
    m = lax.axis_index("mod")
    col_count = obs_days.shape[0] * n_mod
    log_obs = math.log(col_count * lax.axis_size("obs"))
    log_model = math.log(row_count * n_mod)
    blocks = [obs_days] + [
        lax.ppermute(obs_days, "mod", shift_pairs(n_mod, s)) for s in range(1, n_mod)
    ]
    order = (m - jnp.arange(n_mod)) % n_mod
    gathered = jnp.concatenate(blocks, axis=0)
    base_blocks = [pair_scores(model_days, row_square, b) for b in blocks]

    def split(vec):
        return jnp.split(vec, n_mod)

    def row_lse(col_potential):
        parts = []
        for hb, sb in zip(split(col_potential / entropy_scale), base_blocks):
            scores = hb[None, :] + sb
            peaks = jnp.max(scores, axis=1)
            parts.append(peaks + jnp.log(jnp.sum(jnp.exp(scores - peaks[:, None]), axis=1)))
        stacked = jnp.stack(parts)
        top = jnp.max(stacked, axis=0)
        local = top + jnp.log(jnp.sum(jnp.exp(stacked - top[None]), axis=0))
        return lse_across(local, "obs")

    def col_lse(row_potential):
        g = (row_potential / entropy_scale)[:, None]
        parts = []
        for sb in base_blocks:
            col_scores = g + sb
            col_peaks = jnp.max(col_scores, axis=0)
            parts.append(col_peaks + jnp.log(jnp.sum(jnp.exp(col_scores - col_peaks[None, :]), axis=0)))
        return jnp.concatenate(parts)

    col_shift = jnp.zeros((col_count,), jnp.float32)
    for iteration in range(ITERS):
        row_potential = -entropy_scale * (row_lse(col_shift) - log_obs)
        local = col_lse(row_potential)
        col_global = lse_across(reorder(local, order), "mod")
        col_potential = -entropy_scale * (col_global - log_model)
        col_shift = reorder(col_potential, order)
    peaks, local, partial_map = final_local(col_shift / entropy_scale, base_blocks, gathered)
    final_lse = lse_across(local, "obs")
    row_potential = -entropy_scale * (final_lse - log_obs)
    mapped = scatter_obs(partial_map, peaks, final_lse)
    return (mapped, row_potential, col_potential)


def solution(mesh):
    in_specs = (P(("region", "mod"), None), P(("region", "obs", "mod"), None))
    out_specs = (P(("region", "mod", "obs"), None), P(("region", "mod")), P(("region", "obs")))
    return jax.shard_map(
        on_device, mesh=mesh, in_specs=in_specs, out_specs=out_specs, check_vma=False
    )
```

```python
import math

import jax
import jax.numpy as jnp
from jax import lax
from jax.experimental import pallas as pl
from jax.experimental.pallas import tpu as pltpu
from jax.sharding import PartitionSpec as P

ITERS = 2

RB = 8


def _lane_tiles(s):
    return [s[:, j * 128:(j + 1) * 128] for j in range(s.shape[1] // 128)]


def _final_kernel(*refs):
    h_ref = refs[0]
    nb = len(refs) - 9
    c_refs = refs[1:1 + nb]
    y_ref, m_ref, l_ref, p_ref, w_ref, m_scr, t_scr, r_scr = refs[1 + nb:]
    tr = c_refs[0].shape[0]
    width = c_refs[0].shape[1]

    def scores(r):
        return [h_ref[:, k * width:(k + 1) * width] + c[pl.ds(r, RB), :] for k, c in enumerate(c_refs)]

    def p1(i, carry):
        r = pl.multiple_of(i * RB, RB)
        tiles = [t for sc in scores(r) for t in _lane_tiles(sc)]
        m = tiles[0]
        for t in tiles[1:]:
            m = jnp.maximum(m, t)
        m_scr[pl.ds(r, RB), :] = m
        return carry
    lax.fori_loop(0, tr // RB, p1, 0, unroll=4)
    r_scr[...] = jnp.max(m_scr[...], axis=1, keepdims=True)
    m_ref[...] = jnp.max(m_scr[...].T, axis=0, keepdims=True)

    def p2(i, carry):
        r = pl.multiple_of(i * RB, RB)
        mr = r_scr[pl.ds(r, RB), :]
        t = None
        for k, sc in enumerate(scores(r)):
            w = jnp.exp(sc - mr)
            w_ref[pl.ds(r, RB), k * width:(k + 1) * width] = w
            for u in _lane_tiles(w):
                t = u if t is None else t + u
        t_scr[pl.ds(r, RB), :] = t
        return carry
    lax.fori_loop(0, tr // RB, p2, 0, unroll=4)
    l_ref[...] = m_ref[...] + jnp.log(jnp.sum(t_scr[...].T, axis=0, keepdims=True))
    w = w_ref[...]
    wh = w.astype(jnp.bfloat16)
    wl = (w - wh.astype(jnp.float32)).astype(jnp.bfloat16)
    y = y_ref[...]
    yh = y.astype(jnp.bfloat16)
    yl = (y - yh.astype(jnp.float32)).astype(jnp.bfloat16)
    acc = jnp.dot(wh, yh, preferred_element_type=jnp.float32)
    acc = acc + jnp.dot(wh, yl, preferred_element_type=jnp.float32)
    acc = acc + jnp.dot(wl, yh, preferred_element_type=jnp.float32)
    p_ref[...] = acc


def final_local(h, blocks, y, tr=256):
    R, width = blocks[0].shape
    C = width * len(blocks)
    F = y.shape[1]
    m, l, p = pl.pallas_call(
        _final_kernel,
        grid=(R // tr,),
        in_specs=[pl.BlockSpec((1, C), lambda i: (0, 0))]
        + [pl.BlockSpec((tr, width), lambda i: (i, 0)) for _ in blocks]
        + [pl.BlockSpec((C, F), lambda i: (0, 0))],
        out_specs=[pl.BlockSpec((1, tr), lambda i: (0, i)), pl.BlockSpec((1, tr), lambda i: (0, i)),
                   pl.BlockSpec((tr, F), lambda i: (i, 0))],
        out_shape=[jax.ShapeDtypeStruct((1, R), jnp.float32), jax.ShapeDtypeStruct((1, R), jnp.float32),
                   jax.ShapeDtypeStruct((R, F), jnp.float32)],
        scratch_shapes=[pltpu.VMEM((tr, C), jnp.float32), pltpu.VMEM((tr, 128), jnp.float32),
                        pltpu.VMEM((tr, 128), jnp.float32), pltpu.VMEM((tr, 1), jnp.float32)],
    )(h.reshape(1, C), *blocks, y)
    return m.reshape(R), l.reshape(R), p


entropy_scale = 0.02


def shift_pairs(n, s):
    return [(i, (i + s) % n) for i in range(n)]


def pair_scores(block_rows, block_square, columns):
    column_square = jnp.sum(columns * columns, axis=1)
    cross = lax.dot_general(
        block_rows,
        columns,
        (((1,), (1,)), ((), ())),
        precision=lax.Precision.HIGH,
        preferred_element_type=jnp.float32,
    )
    cost = (block_square[:, None] + column_square[None, :] - 2.0 * cross) / block_rows.shape[1]
    return -cost / entropy_scale


def lse_across(local_lse, axis):
    n = lax.axis_size(axis)
    vals = [local_lse] + [lax.ppermute(local_lse, axis, shift_pairs(n, s)) for s in range(1, n)]
    stacked = jnp.stack(vals)
    top = jnp.max(stacked, axis=0)
    return top + jnp.log(jnp.sum(jnp.exp(stacked - top[None]), axis=0))


def reorder(vec, order):
    n = order.shape[0]
    return jnp.take(vec.reshape(n, -1), order, axis=0).reshape(-1)


def scatter_obs(partial, peaks, final_lse):
    n = lax.axis_size("obs")
    half = n // 2
    o = lax.axis_index("obs")
    x = o // 2
    c = o % 2
    share = partial.shape[0] // n
    p4 = partial.reshape(half, 2, share, partial.shape[1])
    m4 = peaks.reshape(half, 2, share)
    keep = lax.dynamic_index_in_dim(p4, c, axis=1, keepdims=False)
    give = lax.dynamic_index_in_dim(p4, 1 - c, axis=1, keepdims=False)
    m_keep = lax.dynamic_index_in_dim(m4, c, axis=1, keepdims=False)
    m_give = lax.dynamic_index_in_dim(m4, 1 - c, axis=1, keepdims=False)
    partner = [(i, i ^ 1) for i in range(n)]
    got = lax.ppermute(give, "obs", partner)
    m_got = lax.ppermute(m_give, "obs", partner)
    top = jnp.maximum(m_keep, m_got)
    acc = keep * jnp.exp(m_keep - top)[..., None] + got * jnp.exp(m_got - top)[..., None]
    pieces = [(lax.dynamic_index_in_dim(acc, x, axis=0, keepdims=False),
               lax.dynamic_index_in_dim(top, x, axis=0, keepdims=False))]
    for k in range(1, half):
        pairs = [(i, ((i // 2 + k) % half) * 2 + i % 2) for i in range(n)]
        j = (x + k) % half
        pieces.append((
            lax.ppermute(lax.dynamic_index_in_dim(acc, j, axis=0, keepdims=False), "obs", pairs),
            lax.ppermute(lax.dynamic_index_in_dim(top, j, axis=0, keepdims=False), "obs", pairs),
        ))
    own_lse = lax.dynamic_slice_in_dim(final_lse, o * share, share)
    total = pieces[0][0] * jnp.exp(pieces[0][1] - own_lse)[:, None]
    for piece, piece_top in pieces[1:]:
        total = total + piece * jnp.exp(piece_top - own_lse)[:, None]
    return total


def on_device(model_days, obs_days):
    row_square = jnp.sum(model_days * model_days, axis=1)
    row_count = model_days.shape[0]
    n_mod = lax.axis_size("mod")
    m = lax.axis_index("mod")
    col_count = obs_days.shape[0] * n_mod
    log_obs = math.log(col_count * lax.axis_size("obs"))
    log_model = math.log(row_count * n_mod)
    blocks = [obs_days] + [
        lax.ppermute(obs_days, "mod", shift_pairs(n_mod, s)) for s in range(1, n_mod)
    ]
    order = (m - jnp.arange(n_mod)) % n_mod
    gathered = jnp.concatenate(blocks, axis=0)
    base_blocks = [pair_scores(model_days, row_square, b) for b in blocks]

    def split(vec):
        return jnp.split(vec, n_mod)

    def row_lse(col_potential):
        parts = []
        for hb, sb in zip(split(col_potential / entropy_scale), base_blocks):
            scores = hb[None, :] + sb
            peaks = jnp.max(scores, axis=1)
            parts.append(peaks + jnp.log(jnp.sum(jnp.exp(scores - peaks[:, None]), axis=1)))
        stacked = jnp.stack(parts)
        top = jnp.max(stacked, axis=0)
        local = top + jnp.log(jnp.sum(jnp.exp(stacked - top[None]), axis=0))
        return lse_across(local, "obs")

    def col_lse(row_potential):
        g = (row_potential / entropy_scale)[:, None]
        parts = []
        for sb in base_blocks:
            col_scores = g + sb
            col_peaks = jnp.max(col_scores, axis=0)
            parts.append(col_peaks + jnp.log(jnp.sum(jnp.exp(col_scores - col_peaks[None, :]), axis=0)))
        return jnp.concatenate(parts)

    col_shift = jnp.zeros((col_count,), jnp.float32)
    for iteration in range(ITERS):
        row_potential = -entropy_scale * (row_lse(col_shift) - log_obs)
        local = col_lse(row_potential)
        col_global = lse_across(reorder(local, order), "mod")
        col_potential = -entropy_scale * (col_global - log_model)
        col_shift = reorder(col_potential, order)
    peaks, local, partial_map = final_local(col_shift / entropy_scale, base_blocks, gathered)
    final_lse = lse_across(local, "obs")
    row_potential = -entropy_scale * (final_lse - log_obs)
    mapped = scatter_obs(partial_map, peaks, final_lse)
    return (mapped, row_potential, col_potential)


def solution(mesh):
    in_specs = (P(("region", "mod"), None), P(("region", "obs", "mod"), None))
    out_specs = (P(("region", "mod", "obs"), None), P(("region", "mod")), P(("region", "obs")))
    return jax.shard_map(
        on_device, mesh=mesh, in_specs=in_specs, out_specs=out_specs, check_vma=False
    )
```

```python
import math

import jax
import jax.numpy as jnp
from jax import lax
from jax.experimental import pallas as pl
from jax.experimental.pallas import tpu as pltpu
from jax.sharding import PartitionSpec as P

ITERS = 2

RB = 8


def _lane_tiles(s):
    return [s[:, j * 128:(j + 1) * 128] for j in range(s.shape[1] // 128)]


def _final_kernel(*refs):
    h_ref = refs[0]
    nb = len(refs) - 9
    c_refs = refs[1:1 + nb]
    y_ref, m_ref, l_ref, p_ref, w_ref, m_scr, t_scr, r_scr = refs[1 + nb:]
    tr = c_refs[0].shape[0]
    width = c_refs[0].shape[1]

    def scores(r):
        return [h_ref[:, k * width:(k + 1) * width] + c[pl.ds(r, RB), :] for k, c in enumerate(c_refs)]

    def p1(i, carry):
        r = pl.multiple_of(i * RB, RB)
        tiles = [t for sc in scores(r) for t in _lane_tiles(sc)]
        m = tiles[0]
        for t in tiles[1:]:
            m = jnp.maximum(m, t)
        m_scr[pl.ds(r, RB), :] = m
        return carry
    lax.fori_loop(0, tr // RB, p1, 0, unroll=4)
    r_scr[...] = jnp.max(m_scr[...], axis=1, keepdims=True)
    m_ref[...] = jnp.max(m_scr[...].T, axis=0, keepdims=True)

    def p2(i, carry):
        r = pl.multiple_of(i * RB, RB)
        mr = r_scr[pl.ds(r, RB), :]
        t = None
        for k, sc in enumerate(scores(r)):
            w = jnp.exp(sc - mr)
            w_ref[pl.ds(r, RB), k * width:(k + 1) * width] = w
            for u in _lane_tiles(w):
                t = u if t is None else t + u
        t_scr[pl.ds(r, RB), :] = t
        return carry
    lax.fori_loop(0, tr // RB, p2, 0, unroll=4)
    l_ref[...] = m_ref[...] + jnp.log(jnp.sum(t_scr[...].T, axis=0, keepdims=True))
    w = w_ref[...]
    wh = w.astype(jnp.bfloat16)
    wl = (w - wh.astype(jnp.float32)).astype(jnp.bfloat16)
    y = y_ref[...]
    yh = y.astype(jnp.bfloat16)
    yl = (y - yh.astype(jnp.float32)).astype(jnp.bfloat16)
    acc = jnp.dot(wh, yh, preferred_element_type=jnp.float32)
    acc = acc + jnp.dot(wh, yl, preferred_element_type=jnp.float32)
    acc = acc + jnp.dot(wl, yh, preferred_element_type=jnp.float32)
    p_ref[...] = acc


def final_local(h, blocks, y, tr=512):
    R, width = blocks[0].shape
    C = width * len(blocks)
    F = y.shape[1]
    m, l, p = pl.pallas_call(
        _final_kernel,
        grid=(R // tr,),
        in_specs=[pl.BlockSpec((1, C), lambda i: (0, 0))]
        + [pl.BlockSpec((tr, width), lambda i: (i, 0)) for _ in blocks]
        + [pl.BlockSpec((C, F), lambda i: (0, 0))],
        out_specs=[pl.BlockSpec((1, tr), lambda i: (0, i)), pl.BlockSpec((1, tr), lambda i: (0, i)),
                   pl.BlockSpec((tr, F), lambda i: (i, 0))],
        out_shape=[jax.ShapeDtypeStruct((1, R), jnp.float32), jax.ShapeDtypeStruct((1, R), jnp.float32),
                   jax.ShapeDtypeStruct((R, F), jnp.float32)],
        scratch_shapes=[pltpu.VMEM((tr, C), jnp.float32), pltpu.VMEM((tr, 128), jnp.float32),
                        pltpu.VMEM((tr, 128), jnp.float32), pltpu.VMEM((tr, 1), jnp.float32)],
    )(h.reshape(1, C), *blocks, y)
    return m.reshape(R), l.reshape(R), p


entropy_scale = 0.02


def shift_pairs(n, s):
    return [(i, (i + s) % n) for i in range(n)]


def pair_scores(block_rows, block_square, columns):
    column_square = jnp.sum(columns * columns, axis=1)
    cross = lax.dot_general(
        block_rows,
        columns,
        (((1,), (1,)), ((), ())),
        precision=lax.Precision.HIGH,
        preferred_element_type=jnp.float32,
    )
    cost = (block_square[:, None] + column_square[None, :] - 2.0 * cross) / block_rows.shape[1]
    return -cost / entropy_scale


def lse_across(local_lse, axis):
    n = lax.axis_size(axis)
    vals = [local_lse] + [lax.ppermute(local_lse, axis, shift_pairs(n, s)) for s in range(1, n)]
    stacked = jnp.stack(vals)
    top = jnp.max(stacked, axis=0)
    return top + jnp.log(jnp.sum(jnp.exp(stacked - top[None]), axis=0))


def reorder(vec, order):
    n = order.shape[0]
    return jnp.take(vec.reshape(n, -1), order, axis=0).reshape(-1)


def scatter_obs(partial, peaks, final_lse):
    n = lax.axis_size("obs")
    half = n // 2
    o = lax.axis_index("obs")
    x = o // 2
    c = o % 2
    share = partial.shape[0] // n
    p4 = partial.reshape(half, 2, share, partial.shape[1])
    m4 = peaks.reshape(half, 2, share)
    keep = lax.dynamic_index_in_dim(p4, c, axis=1, keepdims=False)
    give = lax.dynamic_index_in_dim(p4, 1 - c, axis=1, keepdims=False)
    m_keep = lax.dynamic_index_in_dim(m4, c, axis=1, keepdims=False)
    m_give = lax.dynamic_index_in_dim(m4, 1 - c, axis=1, keepdims=False)
    partner = [(i, i ^ 1) for i in range(n)]
    got = lax.ppermute(give, "obs", partner)
    m_got = lax.ppermute(m_give, "obs", partner)
    top = jnp.maximum(m_keep, m_got)
    acc = keep * jnp.exp(m_keep - top)[..., None] + got * jnp.exp(m_got - top)[..., None]
    pieces = [(lax.dynamic_index_in_dim(acc, x, axis=0, keepdims=False),
               lax.dynamic_index_in_dim(top, x, axis=0, keepdims=False))]
    for k in range(1, half):
        pairs = [(i, ((i // 2 + k) % half) * 2 + i % 2) for i in range(n)]
        j = (x + k) % half
        pieces.append((
            lax.ppermute(lax.dynamic_index_in_dim(acc, j, axis=0, keepdims=False), "obs", pairs),
            lax.ppermute(lax.dynamic_index_in_dim(top, j, axis=0, keepdims=False), "obs", pairs),
        ))
    own_lse = lax.dynamic_slice_in_dim(final_lse, o * share, share)
    total = pieces[0][0] * jnp.exp(pieces[0][1] - own_lse)[:, None]
    for piece, piece_top in pieces[1:]:
        total = total + piece * jnp.exp(piece_top - own_lse)[:, None]
    return total


def on_device(model_days, obs_days):
    row_square = jnp.sum(model_days * model_days, axis=1)
    row_count = model_days.shape[0]
    n_mod = lax.axis_size("mod")
    m = lax.axis_index("mod")
    col_count = obs_days.shape[0] * n_mod
    log_obs = math.log(col_count * lax.axis_size("obs"))
    log_model = math.log(row_count * n_mod)
    blocks = [obs_days] + [
        lax.ppermute(obs_days, "mod", shift_pairs(n_mod, s)) for s in range(1, n_mod)
    ]
    order = (m - jnp.arange(n_mod)) % n_mod
    gathered = jnp.concatenate(blocks, axis=0)
    base_blocks = [pair_scores(model_days, row_square, b) for b in blocks]

    def split(vec):
        return jnp.split(vec, n_mod)

    def row_lse(col_potential):
        parts = []
        for hb, sb in zip(split(col_potential / entropy_scale), base_blocks):
            scores = hb[None, :] + sb
            peaks = jnp.max(scores, axis=1)
            parts.append(peaks + jnp.log(jnp.sum(jnp.exp(scores - peaks[:, None]), axis=1)))
        stacked = jnp.stack(parts)
        top = jnp.max(stacked, axis=0)
        local = top + jnp.log(jnp.sum(jnp.exp(stacked - top[None]), axis=0))
        return lse_across(local, "obs")

    def col_lse(row_potential):
        g = (row_potential / entropy_scale)[:, None]
        parts = []
        for sb in base_blocks:
            col_scores = g + sb
            col_peaks = jnp.max(col_scores, axis=0)
            parts.append(col_peaks + jnp.log(jnp.sum(jnp.exp(col_scores - col_peaks[None, :]), axis=0)))
        return jnp.concatenate(parts)

    col_shift = jnp.zeros((col_count,), jnp.float32)
    for iteration in range(ITERS):
        row_potential = -entropy_scale * (row_lse(col_shift) - log_obs)
        local = col_lse(row_potential)
        col_global = lse_across(reorder(local, order), "mod")
        col_potential = -entropy_scale * (col_global - log_model)
        col_shift = reorder(col_potential, order)
    peaks, local, partial_map = final_local(col_shift / entropy_scale, base_blocks, gathered)
    final_lse = lse_across(local, "obs")
    row_potential = -entropy_scale * (final_lse - log_obs)
    mapped = scatter_obs(partial_map, peaks, final_lse)
    return (mapped, row_potential, col_potential)


def solution(mesh):
    in_specs = (P(("region", "mod"), None), P(("region", "obs", "mod"), None))
    out_specs = (P(("region", "mod", "obs"), None), P(("region", "mod")), P(("region", "obs")))
    return jax.shard_map(
        on_device, mesh=mesh, in_specs=in_specs, out_specs=out_specs, check_vma=False
    )
```

```python
import math

import jax
import jax.numpy as jnp
from jax import lax
from jax.experimental import pallas as pl
from jax.experimental.pallas import tpu as pltpu
from jax.sharding import PartitionSpec as P

ITERS = 2

RB = 8


def _lane_tiles(s):
    return [s[:, j * 128:(j + 1) * 128] for j in range(s.shape[1] // 128)]


def _final_kernel(*refs):
    h_ref = refs[0]
    nb = len(refs) - 9
    c_refs = refs[1:1 + nb]
    y_ref, m_ref, l_ref, p_ref, w_ref, m_scr, t_scr, r_scr = refs[1 + nb:]
    tr = c_refs[0].shape[0]
    width = c_refs[0].shape[1]

    def scores(r):
        return [h_ref[:, k * width:(k + 1) * width] + c[pl.ds(r, RB), :] for k, c in enumerate(c_refs)]

    def p1(i, carry):
        r = pl.multiple_of(i * RB, RB)
        tiles = [t for sc in scores(r) for t in _lane_tiles(sc)]
        m = tiles[0]
        for t in tiles[1:]:
            m = jnp.maximum(m, t)
        m_scr[pl.ds(r, RB), :] = m
        return carry
    lax.fori_loop(0, tr // RB, p1, 0, unroll=4)
    r_scr[...] = jnp.max(m_scr[...], axis=1, keepdims=True)
    m_ref[...] = jnp.max(m_scr[...].T, axis=0, keepdims=True)

    def p2(i, carry):
        r = pl.multiple_of(i * RB, RB)
        mr = r_scr[pl.ds(r, RB), :]
        t = None
        for k, sc in enumerate(scores(r)):
            w = jnp.exp(sc - mr)
            w_ref[pl.ds(r, RB), k * width:(k + 1) * width] = w
            for u in _lane_tiles(w):
                t = u if t is None else t + u
        t_scr[pl.ds(r, RB), :] = t
        return carry
    lax.fori_loop(0, tr // RB, p2, 0, unroll=4)
    l_ref[...] = m_ref[...] + jnp.log(jnp.sum(t_scr[...].T, axis=0, keepdims=True))
    w = w_ref[...]
    wh = w.astype(jnp.bfloat16)
    wl = (w - wh.astype(jnp.float32)).astype(jnp.bfloat16)
    y = y_ref[...]
    yh = y.astype(jnp.bfloat16)
    yl = (y - yh.astype(jnp.float32)).astype(jnp.bfloat16)
    acc = jnp.dot(wh, yh, preferred_element_type=jnp.float32)
    acc = acc + jnp.dot(wh, yl, preferred_element_type=jnp.float32)
    acc = acc + jnp.dot(wl, yh, preferred_element_type=jnp.float32)
    p_ref[...] = acc


def final_local(h, blocks, y, tr=512):
    R, width = blocks[0].shape
    C = width * len(blocks)
    F = y.shape[1]
    m, l, p = pl.pallas_call(
        _final_kernel,
        grid=(R // tr,),
        in_specs=[pl.BlockSpec((1, C), lambda i: (0, 0))]
        + [pl.BlockSpec((tr, width), lambda i: (i, 0)) for _ in blocks]
        + [pl.BlockSpec((C, F), lambda i: (0, 0))],
        out_specs=[pl.BlockSpec((1, tr), lambda i: (0, i)), pl.BlockSpec((1, tr), lambda i: (0, i)),
                   pl.BlockSpec((tr, F), lambda i: (i, 0))],
        out_shape=[jax.ShapeDtypeStruct((1, R), jnp.float32), jax.ShapeDtypeStruct((1, R), jnp.float32),
                   jax.ShapeDtypeStruct((R, F), jnp.float32)],
        scratch_shapes=[pltpu.VMEM((tr, C), jnp.float32), pltpu.VMEM((tr, 128), jnp.float32),
                        pltpu.VMEM((tr, 128), jnp.float32), pltpu.VMEM((tr, 1), jnp.float32)],
    )(h.reshape(1, C), *blocks, y)
    return m.reshape(R), l.reshape(R), p


entropy_scale = 0.02


def shift_pairs(n, s):
    return [(i, (i + s) % n) for i in range(n)]


def pair_scores(block_rows, block_square, columns):
    column_square = jnp.sum(columns * columns, axis=1)
    cross = lax.dot_general(
        block_rows,
        columns,
        (((1,), (1,)), ((), ())),
        precision=lax.Precision.HIGH,
        preferred_element_type=jnp.float32,
    )
    cost = (block_square[:, None] + column_square[None, :] - 2.0 * cross) / block_rows.shape[1]
    return -cost / entropy_scale


def lse_across(local_lse, axis):
    n = lax.axis_size(axis)
    vals = [local_lse] + [lax.ppermute(local_lse, axis, shift_pairs(n, s)) for s in range(1, n)]
    stacked = jnp.stack(vals)
    top = jnp.max(stacked, axis=0)
    return top + jnp.log(jnp.sum(jnp.exp(stacked - top[None]), axis=0))


def reorder(vec, order):
    n = order.shape[0]
    return jnp.take(vec.reshape(n, -1), order, axis=0).reshape(-1)


def scatter_obs(partial, peaks, local):
    n = lax.axis_size("obs")
    half = n // 2
    o = lax.axis_index("obs")
    x = o // 2
    c = o % 2
    share = partial.shape[0] // n
    p4 = partial.reshape(half, 2, share, partial.shape[1])
    m4 = peaks.reshape(half, 2, share)
    keep = lax.dynamic_index_in_dim(p4, c, axis=1, keepdims=False)
    give = lax.dynamic_index_in_dim(p4, 1 - c, axis=1, keepdims=False)
    m_keep = lax.dynamic_index_in_dim(m4, c, axis=1, keepdims=False)
    m_give = lax.dynamic_index_in_dim(m4, 1 - c, axis=1, keepdims=False)
    partner = [(i, i ^ 1) for i in range(n)]
    got = lax.ppermute(give, "obs", partner)
    m_got = lax.ppermute(m_give, "obs", partner)
    top = jnp.maximum(m_keep, m_got)
    acc = keep * jnp.exp(m_keep - top)[..., None] + got * jnp.exp(m_got - top)[..., None]
    acc, top, local = lax.optimization_barrier((acc, top, local))
    final_lse = lse_across(local, "obs")
    pieces = [(lax.dynamic_index_in_dim(acc, x, axis=0, keepdims=False),
               lax.dynamic_index_in_dim(top, x, axis=0, keepdims=False))]
    for k in range(1, half):
        pairs = [(i, ((i // 2 + k) % half) * 2 + i % 2) for i in range(n)]
        j = (x + k) % half
        pieces.append((
            lax.ppermute(lax.dynamic_index_in_dim(acc, j, axis=0, keepdims=False), "obs", pairs),
            lax.ppermute(lax.dynamic_index_in_dim(top, j, axis=0, keepdims=False), "obs", pairs),
        ))
    own_lse = lax.dynamic_slice_in_dim(final_lse, o * share, share)
    total = pieces[0][0] * jnp.exp(pieces[0][1] - own_lse)[:, None]
    for piece, piece_top in pieces[1:]:
        total = total + piece * jnp.exp(piece_top - own_lse)[:, None]
    return total, final_lse


def on_device(model_days, obs_days):
    row_square = jnp.sum(model_days * model_days, axis=1)
    row_count = model_days.shape[0]
    n_mod = lax.axis_size("mod")
    m = lax.axis_index("mod")
    col_count = obs_days.shape[0] * n_mod
    log_obs = math.log(col_count * lax.axis_size("obs"))
    log_model = math.log(row_count * n_mod)
    blocks = [obs_days] + [
        lax.ppermute(obs_days, "mod", shift_pairs(n_mod, s)) for s in range(1, n_mod)
    ]
    order = (m - jnp.arange(n_mod)) % n_mod
    gathered = jnp.concatenate(blocks, axis=0)
    base_blocks = [pair_scores(model_days, row_square, b) for b in blocks]

    def split(vec):
        return jnp.split(vec, n_mod)

    def row_lse(col_potential):
        parts = []
        for hb, sb in zip(split(col_potential / entropy_scale), base_blocks):
            scores = hb[None, :] + sb
            peaks = jnp.max(scores, axis=1)
            parts.append(peaks + jnp.log(jnp.sum(jnp.exp(scores - peaks[:, None]), axis=1)))
        stacked = jnp.stack(parts)
        top = jnp.max(stacked, axis=0)
        local = top + jnp.log(jnp.sum(jnp.exp(stacked - top[None]), axis=0))
        return lse_across(local, "obs")

    def col_lse(row_potential):
        g = (row_potential / entropy_scale)[:, None]
        parts = []
        for sb in base_blocks:
            col_scores = g + sb
            col_peaks = jnp.max(col_scores, axis=0)
            parts.append(col_peaks + jnp.log(jnp.sum(jnp.exp(col_scores - col_peaks[None, :]), axis=0)))
        return jnp.concatenate(parts)

    col_shift = jnp.zeros((col_count,), jnp.float32)
    for iteration in range(ITERS):
        row_potential = -entropy_scale * (row_lse(col_shift) - log_obs)
        local = col_lse(row_potential)
        col_global = lse_across(reorder(local, order), "mod")
        col_potential = -entropy_scale * (col_global - log_model)
        col_shift = reorder(col_potential, order)
    peaks, local, partial_map = final_local(col_shift / entropy_scale, base_blocks, gathered)
    mapped, final_lse = scatter_obs(partial_map, peaks, local)
    row_potential = -entropy_scale * (final_lse - log_obs)
    return (mapped, row_potential, col_potential)


def solution(mesh):
    in_specs = (P(("region", "mod"), None), P(("region", "obs", "mod"), None))
    out_specs = (P(("region", "mod", "obs"), None), P(("region", "mod")), P(("region", "obs")))
    return jax.shard_map(
        on_device, mesh=mesh, in_specs=in_specs, out_specs=out_specs, check_vma=False
    )
```

```python
import math

import jax
import jax.numpy as jnp
from jax import lax
from jax.experimental import pallas as pl
from jax.experimental.pallas import tpu as pltpu
from jax.sharding import PartitionSpec as P

ITERS = 2

RB = 8


def _lane_tiles(s):
    return [s[:, j * 128:(j + 1) * 128] for j in range(s.shape[1] // 128)]


def _final_kernel(*refs):
    h_ref = refs[0]
    nb = len(refs) - 9
    c_refs = refs[1:1 + nb]
    y_ref, m_ref, l_ref, p_ref, w_ref, m_scr, t_scr, r_scr = refs[1 + nb:]
    tr = c_refs[0].shape[0]
    width = c_refs[0].shape[1]

    def scores(r):
        return [h_ref[:, k * width:(k + 1) * width] + c[pl.ds(r, RB), :] for k, c in enumerate(c_refs)]

    def p1(i, carry):
        r = pl.multiple_of(i * RB, RB)
        tiles = [t for sc in scores(r) for t in _lane_tiles(sc)]
        m = tiles[0]
        for t in tiles[1:]:
            m = jnp.maximum(m, t)
        m_scr[pl.ds(r, RB), :] = m
        return carry
    lax.fori_loop(0, tr // RB, p1, 0, unroll=8)
    r_scr[...] = jnp.max(m_scr[...], axis=1, keepdims=True)
    m_ref[...] = jnp.max(m_scr[...].T, axis=0, keepdims=True)

    def p2(i, carry):
        r = pl.multiple_of(i * RB, RB)
        mr = r_scr[pl.ds(r, RB), :]
        t = None
        for k, sc in enumerate(scores(r)):
            w = jnp.exp(sc - mr)
            w_ref[pl.ds(r, RB), k * width:(k + 1) * width] = w
            for u in _lane_tiles(w):
                t = u if t is None else t + u
        t_scr[pl.ds(r, RB), :] = t
        return carry
    lax.fori_loop(0, tr // RB, p2, 0, unroll=8)
    l_ref[...] = m_ref[...] + jnp.log(jnp.sum(t_scr[...].T, axis=0, keepdims=True))
    w = w_ref[...]
    wh = w.astype(jnp.bfloat16)
    wl = (w - wh.astype(jnp.float32)).astype(jnp.bfloat16)
    y = y_ref[...]
    yh = y.astype(jnp.bfloat16)
    yl = (y - yh.astype(jnp.float32)).astype(jnp.bfloat16)
    acc = jnp.dot(wh, yh, preferred_element_type=jnp.float32)
    acc = acc + jnp.dot(wh, yl, preferred_element_type=jnp.float32)
    acc = acc + jnp.dot(wl, yh, preferred_element_type=jnp.float32)
    p_ref[...] = acc


def final_local(h, blocks, y, tr=512):
    R, width = blocks[0].shape
    C = width * len(blocks)
    F = y.shape[1]
    m, l, p = pl.pallas_call(
        _final_kernel,
        grid=(R // tr,),
        in_specs=[pl.BlockSpec((1, C), lambda i: (0, 0))]
        + [pl.BlockSpec((tr, width), lambda i: (i, 0)) for _ in blocks]
        + [pl.BlockSpec((C, F), lambda i: (0, 0))],
        out_specs=[pl.BlockSpec((1, tr), lambda i: (0, i)), pl.BlockSpec((1, tr), lambda i: (0, i)),
                   pl.BlockSpec((tr, F), lambda i: (i, 0))],
        out_shape=[jax.ShapeDtypeStruct((1, R), jnp.float32), jax.ShapeDtypeStruct((1, R), jnp.float32),
                   jax.ShapeDtypeStruct((R, F), jnp.float32)],
        scratch_shapes=[pltpu.VMEM((tr, C), jnp.float32), pltpu.VMEM((tr, 128), jnp.float32),
                        pltpu.VMEM((tr, 128), jnp.float32), pltpu.VMEM((tr, 1), jnp.float32)],
    )(h.reshape(1, C), *blocks, y)
    return m.reshape(R), l.reshape(R), p


entropy_scale = 0.02


def shift_pairs(n, s):
    return [(i, (i + s) % n) for i in range(n)]


def pair_scores(block_rows, block_square, columns):
    column_square = jnp.sum(columns * columns, axis=1)
    cross = lax.dot_general(
        block_rows,
        columns,
        (((1,), (1,)), ((), ())),
        precision=lax.Precision.HIGH,
        preferred_element_type=jnp.float32,
    )
    cost = (block_square[:, None] + column_square[None, :] - 2.0 * cross) / block_rows.shape[1]
    return -cost / entropy_scale


def lse_across(local_lse, axis):
    n = lax.axis_size(axis)
    vals = [local_lse] + [lax.ppermute(local_lse, axis, shift_pairs(n, s)) for s in range(1, n)]
    stacked = jnp.stack(vals)
    top = jnp.max(stacked, axis=0)
    return top + jnp.log(jnp.sum(jnp.exp(stacked - top[None]), axis=0))


def reorder(vec, order):
    n = order.shape[0]
    return jnp.take(vec.reshape(n, -1), order, axis=0).reshape(-1)


def scatter_obs(partial, peaks, local):
    n = lax.axis_size("obs")
    half = n // 2
    o = lax.axis_index("obs")
    x = o // 2
    c = o % 2
    share = partial.shape[0] // n
    p4 = partial.reshape(half, 2, share, partial.shape[1])
    m4 = peaks.reshape(half, 2, share)
    keep = lax.dynamic_index_in_dim(p4, c, axis=1, keepdims=False)
    give = lax.dynamic_index_in_dim(p4, 1 - c, axis=1, keepdims=False)
    m_keep = lax.dynamic_index_in_dim(m4, c, axis=1, keepdims=False)
    m_give = lax.dynamic_index_in_dim(m4, 1 - c, axis=1, keepdims=False)
    partner = [(i, i ^ 1) for i in range(n)]
    got = lax.ppermute(give, "obs", partner)
    m_got = lax.ppermute(m_give, "obs", partner)
    top = jnp.maximum(m_keep, m_got)
    acc = keep * jnp.exp(m_keep - top)[..., None] + got * jnp.exp(m_got - top)[..., None]
    acc, top, local = lax.optimization_barrier((acc, top, local))
    final_lse = lse_across(local, "obs")
    pieces = [(lax.dynamic_index_in_dim(acc, x, axis=0, keepdims=False),
               lax.dynamic_index_in_dim(top, x, axis=0, keepdims=False))]
    for k in range(1, half):
        pairs = [(i, ((i // 2 + k) % half) * 2 + i % 2) for i in range(n)]
        j = (x + k) % half
        pieces.append((
            lax.ppermute(lax.dynamic_index_in_dim(acc, j, axis=0, keepdims=False), "obs", pairs),
            lax.ppermute(lax.dynamic_index_in_dim(top, j, axis=0, keepdims=False), "obs", pairs),
        ))
    own_lse = lax.dynamic_slice_in_dim(final_lse, o * share, share)
    total = pieces[0][0] * jnp.exp(pieces[0][1] - own_lse)[:, None]
    for piece, piece_top in pieces[1:]:
        total = total + piece * jnp.exp(piece_top - own_lse)[:, None]
    return total, final_lse


def on_device(model_days, obs_days):
    row_square = jnp.sum(model_days * model_days, axis=1)
    row_count = model_days.shape[0]
    n_mod = lax.axis_size("mod")
    m = lax.axis_index("mod")
    col_count = obs_days.shape[0] * n_mod
    log_obs = math.log(col_count * lax.axis_size("obs"))
    log_model = math.log(row_count * n_mod)
    blocks = [obs_days] + [
        lax.ppermute(obs_days, "mod", shift_pairs(n_mod, s)) for s in range(1, n_mod)
    ]
    order = (m - jnp.arange(n_mod)) % n_mod
    gathered = jnp.concatenate(blocks, axis=0)
    base_blocks = [pair_scores(model_days, row_square, b) for b in blocks]

    def split(vec):
        return jnp.split(vec, n_mod)

    def row_lse(col_potential):
        parts = []
        for hb, sb in zip(split(col_potential / entropy_scale), base_blocks):
            scores = hb[None, :] + sb
            peaks = jnp.max(scores, axis=1)
            parts.append(peaks + jnp.log(jnp.sum(jnp.exp(scores - peaks[:, None]), axis=1)))
        stacked = jnp.stack(parts)
        top = jnp.max(stacked, axis=0)
        local = top + jnp.log(jnp.sum(jnp.exp(stacked - top[None]), axis=0))
        return lse_across(local, "obs")

    def col_lse(row_potential):
        g = (row_potential / entropy_scale)[:, None]
        parts = []
        for sb in base_blocks:
            col_scores = g + sb
            col_peaks = jnp.max(col_scores, axis=0)
            parts.append(col_peaks + jnp.log(jnp.sum(jnp.exp(col_scores - col_peaks[None, :]), axis=0)))
        return jnp.concatenate(parts)

    col_shift = jnp.zeros((col_count,), jnp.float32)
    for iteration in range(ITERS):
        row_potential = -entropy_scale * (row_lse(col_shift) - log_obs)
        local = col_lse(row_potential)
        col_global = lse_across(reorder(local, order), "mod")
        col_potential = -entropy_scale * (col_global - log_model)
        col_shift = reorder(col_potential, order)
    peaks, local, partial_map = final_local(col_shift / entropy_scale, base_blocks, gathered)
    mapped, final_lse = scatter_obs(partial_map, peaks, local)
    row_potential = -entropy_scale * (final_lse - log_obs)
    return (mapped, row_potential, col_potential)


def solution(mesh):
    in_specs = (P(("region", "mod"), None), P(("region", "obs", "mod"), None))
    out_specs = (P(("region", "mod", "obs"), None), P(("region", "mod")), P(("region", "obs")))
    return jax.shard_map(
        on_device, mesh=mesh, in_specs=in_specs, out_specs=out_specs, check_vma=False
    )
```

```python
import math

import jax
import jax.numpy as jnp
from jax import lax
from jax.experimental import pallas as pl
from jax.experimental.pallas import tpu as pltpu
from jax.sharding import PartitionSpec as P

ITERS = 2

RB = 8


def _lane_tiles(s):
    return [s[:, j * 128:(j + 1) * 128] for j in range(s.shape[1] // 128)]


def _final_kernel(*refs):
    h_ref = refs[0]
    nb = len(refs) - 9
    c_refs = refs[1:1 + nb]
    y_ref, m_ref, l_ref, p_ref, w_ref, m_scr, t_scr, r_scr = refs[1 + nb:]
    tr = c_refs[0].shape[0]
    width = c_refs[0].shape[1]

    def scores(r):
        return [h_ref[:, k * width:(k + 1) * width] + c[pl.ds(r, RB), :] for k, c in enumerate(c_refs)]

    def p1(i, carry):
        r = pl.multiple_of(i * RB, RB)
        tiles = [t for sc in scores(r) for t in _lane_tiles(sc)]
        m = tiles[0]
        for t in tiles[1:]:
            m = jnp.maximum(m, t)
        m_scr[pl.ds(r, RB), :] = m
        return carry
    lax.fori_loop(0, tr // RB, p1, 0, unroll=16)
    r_scr[...] = jnp.max(m_scr[...], axis=1, keepdims=True)
    m_ref[...] = jnp.max(m_scr[...].T, axis=0, keepdims=True)

    def p2(i, carry):
        r = pl.multiple_of(i * RB, RB)
        mr = r_scr[pl.ds(r, RB), :]
        t = None
        for k, sc in enumerate(scores(r)):
            w = jnp.exp(sc - mr)
            w_ref[pl.ds(r, RB), k * width:(k + 1) * width] = w
            for u in _lane_tiles(w):
                t = u if t is None else t + u
        t_scr[pl.ds(r, RB), :] = t
        return carry
    lax.fori_loop(0, tr // RB, p2, 0, unroll=16)
    l_ref[...] = m_ref[...] + jnp.log(jnp.sum(t_scr[...].T, axis=0, keepdims=True))
    w = w_ref[...]
    wh = w.astype(jnp.bfloat16)
    wl = (w - wh.astype(jnp.float32)).astype(jnp.bfloat16)
    y = y_ref[...]
    yh = y.astype(jnp.bfloat16)
    yl = (y - yh.astype(jnp.float32)).astype(jnp.bfloat16)
    acc = jnp.dot(wh, yh, preferred_element_type=jnp.float32)
    acc = acc + jnp.dot(wh, yl, preferred_element_type=jnp.float32)
    acc = acc + jnp.dot(wl, yh, preferred_element_type=jnp.float32)
    p_ref[...] = acc


def final_local(h, blocks, y, tr=512):
    R, width = blocks[0].shape
    C = width * len(blocks)
    F = y.shape[1]
    m, l, p = pl.pallas_call(
        _final_kernel,
        grid=(R // tr,),
        in_specs=[pl.BlockSpec((1, C), lambda i: (0, 0))]
        + [pl.BlockSpec((tr, width), lambda i: (i, 0)) for _ in blocks]
        + [pl.BlockSpec((C, F), lambda i: (0, 0))],
        out_specs=[pl.BlockSpec((1, tr), lambda i: (0, i)), pl.BlockSpec((1, tr), lambda i: (0, i)),
                   pl.BlockSpec((tr, F), lambda i: (i, 0))],
        out_shape=[jax.ShapeDtypeStruct((1, R), jnp.float32), jax.ShapeDtypeStruct((1, R), jnp.float32),
                   jax.ShapeDtypeStruct((R, F), jnp.float32)],
        scratch_shapes=[pltpu.VMEM((tr, C), jnp.float32), pltpu.VMEM((tr, 128), jnp.float32),
                        pltpu.VMEM((tr, 128), jnp.float32), pltpu.VMEM((tr, 1), jnp.float32)],
    )(h.reshape(1, C), *blocks, y)
    return m.reshape(R), l.reshape(R), p


entropy_scale = 0.02


def shift_pairs(n, s):
    return [(i, (i + s) % n) for i in range(n)]


def pair_scores(block_rows, block_square, columns):
    column_square = jnp.sum(columns * columns, axis=1)
    cross = lax.dot_general(
        block_rows,
        columns,
        (((1,), (1,)), ((), ())),
        precision=lax.Precision.HIGH,
        preferred_element_type=jnp.float32,
    )
    cost = (block_square[:, None] + column_square[None, :] - 2.0 * cross) / block_rows.shape[1]
    return -cost / entropy_scale


def lse_across(local_lse, axis):
    n = lax.axis_size(axis)
    vals = [local_lse] + [lax.ppermute(local_lse, axis, shift_pairs(n, s)) for s in range(1, n)]
    stacked = jnp.stack(vals)
    top = jnp.max(stacked, axis=0)
    return top + jnp.log(jnp.sum(jnp.exp(stacked - top[None]), axis=0))


def reorder(vec, order):
    n = order.shape[0]
    return jnp.take(vec.reshape(n, -1), order, axis=0).reshape(-1)


def scatter_obs(partial, peaks, local):
    n = lax.axis_size("obs")
    half = n // 2
    o = lax.axis_index("obs")
    x = o // 2
    c = o % 2
    share = partial.shape[0] // n
    p4 = partial.reshape(half, 2, share, partial.shape[1])
    m4 = peaks.reshape(half, 2, share)
    keep = lax.dynamic_index_in_dim(p4, c, axis=1, keepdims=False)
    give = lax.dynamic_index_in_dim(p4, 1 - c, axis=1, keepdims=False)
    m_keep = lax.dynamic_index_in_dim(m4, c, axis=1, keepdims=False)
    m_give = lax.dynamic_index_in_dim(m4, 1 - c, axis=1, keepdims=False)
    partner = [(i, i ^ 1) for i in range(n)]
    got = lax.ppermute(give, "obs", partner)
    m_got = lax.ppermute(m_give, "obs", partner)
    top = jnp.maximum(m_keep, m_got)
    acc = keep * jnp.exp(m_keep - top)[..., None] + got * jnp.exp(m_got - top)[..., None]
    acc, top, local = lax.optimization_barrier((acc, top, local))
    final_lse = lse_across(local, "obs")
    pieces = [(lax.dynamic_index_in_dim(acc, x, axis=0, keepdims=False),
               lax.dynamic_index_in_dim(top, x, axis=0, keepdims=False))]
    for k in range(1, half):
        pairs = [(i, ((i // 2 + k) % half) * 2 + i % 2) for i in range(n)]
        j = (x + k) % half
        pieces.append((
            lax.ppermute(lax.dynamic_index_in_dim(acc, j, axis=0, keepdims=False), "obs", pairs),
            lax.ppermute(lax.dynamic_index_in_dim(top, j, axis=0, keepdims=False), "obs", pairs),
        ))
    own_lse = lax.dynamic_slice_in_dim(final_lse, o * share, share)
    total = pieces[0][0] * jnp.exp(pieces[0][1] - own_lse)[:, None]
    for piece, piece_top in pieces[1:]:
        total = total + piece * jnp.exp(piece_top - own_lse)[:, None]
    return total, final_lse


def on_device(model_days, obs_days):
    row_square = jnp.sum(model_days * model_days, axis=1)
    row_count = model_days.shape[0]
    n_mod = lax.axis_size("mod")
    m = lax.axis_index("mod")
    col_count = obs_days.shape[0] * n_mod
    log_obs = math.log(col_count * lax.axis_size("obs"))
    log_model = math.log(row_count * n_mod)
    blocks = [obs_days] + [
        lax.ppermute(obs_days, "mod", shift_pairs(n_mod, s)) for s in range(1, n_mod)
    ]
    order = (m - jnp.arange(n_mod)) % n_mod
    gathered = jnp.concatenate(blocks, axis=0)
    base_blocks = [pair_scores(model_days, row_square, b) for b in blocks]

    def split(vec):
        return jnp.split(vec, n_mod)

    def row_lse(col_potential):
        parts = []
        for hb, sb in zip(split(col_potential / entropy_scale), base_blocks):
            scores = hb[None, :] + sb
            peaks = jnp.max(scores, axis=1)
            parts.append(peaks + jnp.log(jnp.sum(jnp.exp(scores - peaks[:, None]), axis=1)))
        stacked = jnp.stack(parts)
        top = jnp.max(stacked, axis=0)
        local = top + jnp.log(jnp.sum(jnp.exp(stacked - top[None]), axis=0))
        return lse_across(local, "obs")

    def col_lse(row_potential):
        g = (row_potential / entropy_scale)[:, None]
        parts = []
        for sb in base_blocks:
            col_scores = g + sb
            col_peaks = jnp.max(col_scores, axis=0)
            parts.append(col_peaks + jnp.log(jnp.sum(jnp.exp(col_scores - col_peaks[None, :]), axis=0)))
        return jnp.concatenate(parts)

    col_shift = jnp.zeros((col_count,), jnp.float32)
    for iteration in range(ITERS):
        row_potential = -entropy_scale * (row_lse(col_shift) - log_obs)
        local = col_lse(row_potential)
        col_global = lse_across(reorder(local, order), "mod")
        col_potential = -entropy_scale * (col_global - log_model)
        col_shift = reorder(col_potential, order)
    peaks, local, partial_map = final_local(col_shift / entropy_scale, base_blocks, gathered)
    mapped, final_lse = scatter_obs(partial_map, peaks, local)
    row_potential = -entropy_scale * (final_lse - log_obs)
    return (mapped, row_potential, col_potential)


def solution(mesh):
    in_specs = (P(("region", "mod"), None), P(("region", "obs", "mod"), None))
    out_specs = (P(("region", "mod", "obs"), None), P(("region", "mod")), P(("region", "obs")))
    return jax.shard_map(
        on_device, mesh=mesh, in_specs=in_specs, out_specs=out_specs, check_vma=False
    )
```

```python
import math

import jax
import jax.numpy as jnp
from jax import lax
from jax.experimental import pallas as pl
from jax.experimental.pallas import tpu as pltpu
from jax.sharding import PartitionSpec as P

ITERS = 2

RB = 8


def _lane_tiles(s):
    return [s[:, j * 128:(j + 1) * 128] for j in range(s.shape[1] // 128)]


def _final_kernel(*refs):
    h_ref = refs[0]
    nb = len(refs) - 9
    c_refs = refs[1:1 + nb]
    y_ref, m_ref, l_ref, p_ref, w_ref, m_scr, t_scr, r_scr = refs[1 + nb:]
    tr = c_refs[0].shape[0]
    width = c_refs[0].shape[1]

    def scores(r):
        return [h_ref[:, k * width:(k + 1) * width] + c[pl.ds(r, RB), :] for k, c in enumerate(c_refs)]

    def p1(i, carry):
        r = pl.multiple_of(i * RB, RB)
        tiles = [t for sc in scores(r) for t in _lane_tiles(sc)]
        m = tiles[0]
        for t in tiles[1:]:
            m = jnp.maximum(m, t)
        m_scr[pl.ds(r, RB), :] = m
        return carry
    lax.fori_loop(0, tr // RB, p1, 0, unroll=32)
    r_scr[...] = jnp.max(m_scr[...], axis=1, keepdims=True)
    m_ref[...] = jnp.max(m_scr[...].T, axis=0, keepdims=True)

    def p2(i, carry):
        r = pl.multiple_of(i * RB, RB)
        mr = r_scr[pl.ds(r, RB), :]
        t = None
        for k, sc in enumerate(scores(r)):
            w = jnp.exp(sc - mr)
            w_ref[pl.ds(r, RB), k * width:(k + 1) * width] = w
            for u in _lane_tiles(w):
                t = u if t is None else t + u
        t_scr[pl.ds(r, RB), :] = t
        return carry
    lax.fori_loop(0, tr // RB, p2, 0, unroll=32)
    l_ref[...] = m_ref[...] + jnp.log(jnp.sum(t_scr[...].T, axis=0, keepdims=True))
    w = w_ref[...]
    wh = w.astype(jnp.bfloat16)
    wl = (w - wh.astype(jnp.float32)).astype(jnp.bfloat16)
    y = y_ref[...]
    yh = y.astype(jnp.bfloat16)
    yl = (y - yh.astype(jnp.float32)).astype(jnp.bfloat16)
    acc = jnp.dot(wh, yh, preferred_element_type=jnp.float32)
    acc = acc + jnp.dot(wh, yl, preferred_element_type=jnp.float32)
    acc = acc + jnp.dot(wl, yh, preferred_element_type=jnp.float32)
    p_ref[...] = acc


def final_local(h, blocks, y, tr=512):
    R, width = blocks[0].shape
    C = width * len(blocks)
    F = y.shape[1]
    m, l, p = pl.pallas_call(
        _final_kernel,
        grid=(R // tr,),
        in_specs=[pl.BlockSpec((1, C), lambda i: (0, 0))]
        + [pl.BlockSpec((tr, width), lambda i: (i, 0)) for _ in blocks]
        + [pl.BlockSpec((C, F), lambda i: (0, 0))],
        out_specs=[pl.BlockSpec((1, tr), lambda i: (0, i)), pl.BlockSpec((1, tr), lambda i: (0, i)),
                   pl.BlockSpec((tr, F), lambda i: (i, 0))],
        out_shape=[jax.ShapeDtypeStruct((1, R), jnp.float32), jax.ShapeDtypeStruct((1, R), jnp.float32),
                   jax.ShapeDtypeStruct((R, F), jnp.float32)],
        scratch_shapes=[pltpu.VMEM((tr, C), jnp.float32), pltpu.VMEM((tr, 128), jnp.float32),
                        pltpu.VMEM((tr, 128), jnp.float32), pltpu.VMEM((tr, 1), jnp.float32)],
    )(h.reshape(1, C), *blocks, y)
    return m.reshape(R), l.reshape(R), p


entropy_scale = 0.02


def shift_pairs(n, s):
    return [(i, (i + s) % n) for i in range(n)]


def pair_scores(block_rows, block_square, columns):
    column_square = jnp.sum(columns * columns, axis=1)
    cross = lax.dot_general(
        block_rows,
        columns,
        (((1,), (1,)), ((), ())),
        precision=lax.Precision.HIGH,
        preferred_element_type=jnp.float32,
    )
    cost = (block_square[:, None] + column_square[None, :] - 2.0 * cross) / block_rows.shape[1]
    return -cost / entropy_scale


def lse_across(local_lse, axis):
    n = lax.axis_size(axis)
    vals = [local_lse] + [lax.ppermute(local_lse, axis, shift_pairs(n, s)) for s in range(1, n)]
    stacked = jnp.stack(vals)
    top = jnp.max(stacked, axis=0)
    return top + jnp.log(jnp.sum(jnp.exp(stacked - top[None]), axis=0))


def reorder(vec, order):
    n = order.shape[0]
    return jnp.take(vec.reshape(n, -1), order, axis=0).reshape(-1)


def scatter_obs(partial, peaks, local):
    n = lax.axis_size("obs")
    half = n // 2
    o = lax.axis_index("obs")
    x = o // 2
    c = o % 2
    share = partial.shape[0] // n
    p4 = partial.reshape(half, 2, share, partial.shape[1])
    m4 = peaks.reshape(half, 2, share)
    keep = lax.dynamic_index_in_dim(p4, c, axis=1, keepdims=False)
    give = lax.dynamic_index_in_dim(p4, 1 - c, axis=1, keepdims=False)
    m_keep = lax.dynamic_index_in_dim(m4, c, axis=1, keepdims=False)
    m_give = lax.dynamic_index_in_dim(m4, 1 - c, axis=1, keepdims=False)
    partner = [(i, i ^ 1) for i in range(n)]
    got = lax.ppermute(give, "obs", partner)
    m_got = lax.ppermute(m_give, "obs", partner)
    top = jnp.maximum(m_keep, m_got)
    acc = keep * jnp.exp(m_keep - top)[..., None] + got * jnp.exp(m_got - top)[..., None]
    acc, top, local = lax.optimization_barrier((acc, top, local))
    final_lse = lse_across(local, "obs")
    pieces = [(lax.dynamic_index_in_dim(acc, x, axis=0, keepdims=False),
               lax.dynamic_index_in_dim(top, x, axis=0, keepdims=False))]
    for k in range(1, half):
        pairs = [(i, ((i // 2 + k) % half) * 2 + i % 2) for i in range(n)]
        j = (x + k) % half
        pieces.append((
            lax.ppermute(lax.dynamic_index_in_dim(acc, j, axis=0, keepdims=False), "obs", pairs),
            lax.ppermute(lax.dynamic_index_in_dim(top, j, axis=0, keepdims=False), "obs", pairs),
        ))
    own_lse = lax.dynamic_slice_in_dim(final_lse, o * share, share)
    total = pieces[0][0] * jnp.exp(pieces[0][1] - own_lse)[:, None]
    for piece, piece_top in pieces[1:]:
        total = total + piece * jnp.exp(piece_top - own_lse)[:, None]
    return total, final_lse


def on_device(model_days, obs_days):
    row_square = jnp.sum(model_days * model_days, axis=1)
    row_count = model_days.shape[0]
    n_mod = lax.axis_size("mod")
    m = lax.axis_index("mod")
    col_count = obs_days.shape[0] * n_mod
    log_obs = math.log(col_count * lax.axis_size("obs"))
    log_model = math.log(row_count * n_mod)
    blocks = [obs_days] + [
        lax.ppermute(obs_days, "mod", shift_pairs(n_mod, s)) for s in range(1, n_mod)
    ]
    order = (m - jnp.arange(n_mod)) % n_mod
    gathered = jnp.concatenate(blocks, axis=0)
    base_blocks = [pair_scores(model_days, row_square, b) for b in blocks]

    def split(vec):
        return jnp.split(vec, n_mod)

    def row_lse(col_potential):
        parts = []
        for hb, sb in zip(split(col_potential / entropy_scale), base_blocks):
            scores = hb[None, :] + sb
            peaks = jnp.max(scores, axis=1)
            parts.append(peaks + jnp.log(jnp.sum(jnp.exp(scores - peaks[:, None]), axis=1)))
        stacked = jnp.stack(parts)
        top = jnp.max(stacked, axis=0)
        local = top + jnp.log(jnp.sum(jnp.exp(stacked - top[None]), axis=0))
        return lse_across(local, "obs")

    def col_lse(row_potential):
        g = (row_potential / entropy_scale)[:, None]
        parts = []
        for sb in base_blocks:
            col_scores = g + sb
            col_peaks = jnp.max(col_scores, axis=0)
            parts.append(col_peaks + jnp.log(jnp.sum(jnp.exp(col_scores - col_peaks[None, :]), axis=0)))
        return jnp.concatenate(parts)

    col_shift = jnp.zeros((col_count,), jnp.float32)
    for iteration in range(ITERS):
        row_potential = -entropy_scale * (row_lse(col_shift) - log_obs)
        local = col_lse(row_potential)
        col_global = lse_across(reorder(local, order), "mod")
        col_potential = -entropy_scale * (col_global - log_model)
        col_shift = reorder(col_potential, order)
    peaks, local, partial_map = final_local(col_shift / entropy_scale, base_blocks, gathered)
    mapped, final_lse = scatter_obs(partial_map, peaks, local)
    row_potential = -entropy_scale * (final_lse - log_obs)
    return (mapped, row_potential, col_potential)


def solution(mesh):
    in_specs = (P(("region", "mod"), None), P(("region", "obs", "mod"), None))
    out_specs = (P(("region", "mod", "obs"), None), P(("region", "mod")), P(("region", "obs")))
    return jax.shard_map(
        on_device, mesh=mesh, in_specs=in_specs, out_specs=out_specs, check_vma=False
    )
```

```python
import math

import jax
import jax.numpy as jnp
from jax import lax
from jax.experimental import pallas as pl
from jax.experimental.pallas import tpu as pltpu
from jax.sharding import PartitionSpec as P

ITERS = 2

RB = 16


def _lane_tiles(s):
    return [s[:, j * 128:(j + 1) * 128] for j in range(s.shape[1] // 128)]


def _final_kernel(*refs):
    h_ref = refs[0]
    nb = len(refs) - 9
    c_refs = refs[1:1 + nb]
    y_ref, m_ref, l_ref, p_ref, w_ref, m_scr, t_scr, r_scr = refs[1 + nb:]
    tr = c_refs[0].shape[0]
    width = c_refs[0].shape[1]

    def scores(r):
        return [h_ref[:, k * width:(k + 1) * width] + c[pl.ds(r, RB), :] for k, c in enumerate(c_refs)]

    def p1(i, carry):
        r = pl.multiple_of(i * RB, RB)
        tiles = [t for sc in scores(r) for t in _lane_tiles(sc)]
        m = tiles[0]
        for t in tiles[1:]:
            m = jnp.maximum(m, t)
        m_scr[pl.ds(r, RB), :] = m
        return carry
    lax.fori_loop(0, tr // RB, p1, 0, unroll=16)
    r_scr[...] = jnp.max(m_scr[...], axis=1, keepdims=True)
    m_ref[...] = jnp.max(m_scr[...].T, axis=0, keepdims=True)

    def p2(i, carry):
        r = pl.multiple_of(i * RB, RB)
        mr = r_scr[pl.ds(r, RB), :]
        t = None
        for k, sc in enumerate(scores(r)):
            w = jnp.exp(sc - mr)
            w_ref[pl.ds(r, RB), k * width:(k + 1) * width] = w
            for u in _lane_tiles(w):
                t = u if t is None else t + u
        t_scr[pl.ds(r, RB), :] = t
        return carry
    lax.fori_loop(0, tr // RB, p2, 0, unroll=16)
    l_ref[...] = m_ref[...] + jnp.log(jnp.sum(t_scr[...].T, axis=0, keepdims=True))
    w = w_ref[...]
    wh = w.astype(jnp.bfloat16)
    wl = (w - wh.astype(jnp.float32)).astype(jnp.bfloat16)
    y = y_ref[...]
    yh = y.astype(jnp.bfloat16)
    yl = (y - yh.astype(jnp.float32)).astype(jnp.bfloat16)
    acc = jnp.dot(wh, yh, preferred_element_type=jnp.float32)
    acc = acc + jnp.dot(wh, yl, preferred_element_type=jnp.float32)
    acc = acc + jnp.dot(wl, yh, preferred_element_type=jnp.float32)
    p_ref[...] = acc


def final_local(h, blocks, y, tr=512):
    R, width = blocks[0].shape
    C = width * len(blocks)
    F = y.shape[1]
    m, l, p = pl.pallas_call(
        _final_kernel,
        grid=(R // tr,),
        in_specs=[pl.BlockSpec((1, C), lambda i: (0, 0))]
        + [pl.BlockSpec((tr, width), lambda i: (i, 0)) for _ in blocks]
        + [pl.BlockSpec((C, F), lambda i: (0, 0))],
        out_specs=[pl.BlockSpec((1, tr), lambda i: (0, i)), pl.BlockSpec((1, tr), lambda i: (0, i)),
                   pl.BlockSpec((tr, F), lambda i: (i, 0))],
        out_shape=[jax.ShapeDtypeStruct((1, R), jnp.float32), jax.ShapeDtypeStruct((1, R), jnp.float32),
                   jax.ShapeDtypeStruct((R, F), jnp.float32)],
        scratch_shapes=[pltpu.VMEM((tr, C), jnp.float32), pltpu.VMEM((tr, 128), jnp.float32),
                        pltpu.VMEM((tr, 128), jnp.float32), pltpu.VMEM((tr, 1), jnp.float32)],
    )(h.reshape(1, C), *blocks, y)
    return m.reshape(R), l.reshape(R), p


entropy_scale = 0.02


def shift_pairs(n, s):
    return [(i, (i + s) % n) for i in range(n)]


def pair_scores(block_rows, block_square, columns):
    column_square = jnp.sum(columns * columns, axis=1)
    cross = lax.dot_general(
        block_rows,
        columns,
        (((1,), (1,)), ((), ())),
        precision=lax.Precision.HIGH,
        preferred_element_type=jnp.float32,
    )
    cost = (block_square[:, None] + column_square[None, :] - 2.0 * cross) / block_rows.shape[1]
    return -cost / entropy_scale


def lse_across(local_lse, axis):
    n = lax.axis_size(axis)
    vals = [local_lse] + [lax.ppermute(local_lse, axis, shift_pairs(n, s)) for s in range(1, n)]
    stacked = jnp.stack(vals)
    top = jnp.max(stacked, axis=0)
    return top + jnp.log(jnp.sum(jnp.exp(stacked - top[None]), axis=0))


def reorder(vec, order):
    n = order.shape[0]
    return jnp.take(vec.reshape(n, -1), order, axis=0).reshape(-1)


def scatter_obs(partial, peaks, local):
    n = lax.axis_size("obs")
    half = n // 2
    o = lax.axis_index("obs")
    x = o // 2
    c = o % 2
    share = partial.shape[0] // n
    p4 = partial.reshape(half, 2, share, partial.shape[1])
    m4 = peaks.reshape(half, 2, share)
    keep = lax.dynamic_index_in_dim(p4, c, axis=1, keepdims=False)
    give = lax.dynamic_index_in_dim(p4, 1 - c, axis=1, keepdims=False)
    m_keep = lax.dynamic_index_in_dim(m4, c, axis=1, keepdims=False)
    m_give = lax.dynamic_index_in_dim(m4, 1 - c, axis=1, keepdims=False)
    partner = [(i, i ^ 1) for i in range(n)]
    got = lax.ppermute(give, "obs", partner)
    m_got = lax.ppermute(m_give, "obs", partner)
    top = jnp.maximum(m_keep, m_got)
    acc = keep * jnp.exp(m_keep - top)[..., None] + got * jnp.exp(m_got - top)[..., None]
    acc, top, local = lax.optimization_barrier((acc, top, local))
    final_lse = lse_across(local, "obs")
    pieces = [(lax.dynamic_index_in_dim(acc, x, axis=0, keepdims=False),
               lax.dynamic_index_in_dim(top, x, axis=0, keepdims=False))]
    for k in range(1, half):
        pairs = [(i, ((i // 2 + k) % half) * 2 + i % 2) for i in range(n)]
        j = (x + k) % half
        pieces.append((
            lax.ppermute(lax.dynamic_index_in_dim(acc, j, axis=0, keepdims=False), "obs", pairs),
            lax.ppermute(lax.dynamic_index_in_dim(top, j, axis=0, keepdims=False), "obs", pairs),
        ))
    own_lse = lax.dynamic_slice_in_dim(final_lse, o * share, share)
    total = pieces[0][0] * jnp.exp(pieces[0][1] - own_lse)[:, None]
    for piece, piece_top in pieces[1:]:
        total = total + piece * jnp.exp(piece_top - own_lse)[:, None]
    return total, final_lse


def on_device(model_days, obs_days):
    row_square = jnp.sum(model_days * model_days, axis=1)
    row_count = model_days.shape[0]
    n_mod = lax.axis_size("mod")
    m = lax.axis_index("mod")
    col_count = obs_days.shape[0] * n_mod
    log_obs = math.log(col_count * lax.axis_size("obs"))
    log_model = math.log(row_count * n_mod)
    blocks = [obs_days] + [
        lax.ppermute(obs_days, "mod", shift_pairs(n_mod, s)) for s in range(1, n_mod)
    ]
    order = (m - jnp.arange(n_mod)) % n_mod
    gathered = jnp.concatenate(blocks, axis=0)
    base_blocks = [pair_scores(model_days, row_square, b) for b in blocks]

    def split(vec):
        return jnp.split(vec, n_mod)

    def row_lse(col_potential):
        parts = []
        for hb, sb in zip(split(col_potential / entropy_scale), base_blocks):
            scores = hb[None, :] + sb
            peaks = jnp.max(scores, axis=1)
            parts.append(peaks + jnp.log(jnp.sum(jnp.exp(scores - peaks[:, None]), axis=1)))
        stacked = jnp.stack(parts)
        top = jnp.max(stacked, axis=0)
        local = top + jnp.log(jnp.sum(jnp.exp(stacked - top[None]), axis=0))
        return lse_across(local, "obs")

    def col_lse(row_potential):
        g = (row_potential / entropy_scale)[:, None]
        parts = []
        for sb in base_blocks:
            col_scores = g + sb
            col_peaks = jnp.max(col_scores, axis=0)
            parts.append(col_peaks + jnp.log(jnp.sum(jnp.exp(col_scores - col_peaks[None, :]), axis=0)))
        return jnp.concatenate(parts)

    col_shift = jnp.zeros((col_count,), jnp.float32)
    for iteration in range(ITERS):
        row_potential = -entropy_scale * (row_lse(col_shift) - log_obs)
        local = col_lse(row_potential)
        col_global = lse_across(reorder(local, order), "mod")
        col_potential = -entropy_scale * (col_global - log_model)
        col_shift = reorder(col_potential, order)
    peaks, local, partial_map = final_local(col_shift / entropy_scale, base_blocks, gathered)
    mapped, final_lse = scatter_obs(partial_map, peaks, local)
    row_potential = -entropy_scale * (final_lse - log_obs)
    return (mapped, row_potential, col_potential)


def solution(mesh):
    in_specs = (P(("region", "mod"), None), P(("region", "obs", "mod"), None))
    out_specs = (P(("region", "mod", "obs"), None), P(("region", "mod")), P(("region", "obs")))
    return jax.shard_map(
        on_device, mesh=mesh, in_specs=in_specs, out_specs=out_specs, check_vma=False
    )
```
